256 devices in a mesh: blk: 32 (over y, x, z_hi), grp: 8 (over z_lo, core).
Axes of the slice: x: 4, y: 4, z: 8 (z_hi: 2, z_lo: 4; z = z_hi * 4 + z_lo), core: 2. Of those that a mesh axis runs over, the one named last changes fastest.
Arguments:
- x_blocks: bfloat16 [4096, 128, 128], P(('blk', 'grp')), may hold values from -0.59765625 to 0.59765625
- pair_left: int32 [32, 8, 32, 12], P('blk', 'grp'), may hold values from 0 to 127
- pair_right: int32 [32, 8, 32, 12], P('blk', 'grp'), may hold values from 0 to 127
- pair_target: int32 [32, 8, 32, 12], P('blk', 'grp'), may hold values from 0 to 3
Outputs:
- c_blocks: bfloat16 [32, 8, 4, 128, 128], P('blk', 'grp')
The draws below stay inside these ranges and needn't reach their ends.
All inputs are finite; a program needn't handle non-finite values.
Results may differ from the reference program's by a relative error of at most 0.001.
Values may be sent and summed in bfloat16 or wider, within the bound.
No kernel may reach another device: no remote copies, remote signals or barrier semaphores. Data moves between devices by JAX's collectives and lax.ppermute only.
A program may use at most 64 MiB of HBM per device.

```python
import jax
import jax.numpy as jnp
from jax import lax

BS = 128
NB = 16
PAIRS = 12
CS = 4
CYCLE = 32
GROUP = 8
BLOCKS = 4096


def with_ends(entries, rng, least, top_value):
    shape = entries.shape
    spot = [jax.random.randint(jax.random.fold_in(rng, axis), (), 0, shape[axis]) for axis in range(len(shape))]
    entries = entries.at[tuple(spot)].set(least)
    longest = shape.index(max(shape))
    spot[longest] = (spot[longest] + 1) % shape[longest]
    return entries.at[tuple(spot)].set(top_value)


def shard_levels(stream_key, dims, split, least, largest):
    gain = 1.0
    for dim, parts in split:
        draws = jax.random.uniform(jax.random.fold_in(jax.random.fold_in(stream_key, 6), dim), (parts,), jnp.float32, least / len(split), largest / len(split))
        gain = gain * jnp.repeat(jnp.exp(draws), dims[dim] // parts).reshape((-1,) + (1,) * (len(dims) - 1 - dim))
    return gain


def gaussian(stream_key, dims, spread, most, split=(), kind=jnp.bfloat16):
    entries = jax.random.normal(stream_key, dims, jnp.float32) * spread
    if len(split) > 0:
        entries = shard_levels(stream_key, dims, split, -0.22, 0.18) * entries
    return jnp.clip(entries, min=-most, max=most).astype(kind)


def setup_inputs(seed: int = 0) -> dict:
    arg_keys = jax.random.split(jax.random.key(seed), 5)
    x_blocks = gaussian(arg_keys[0], (BLOCKS, BS, BS), 0.1, 0.59765625, ((0, 256),))
    pair_left = with_ends(jax.random.randint(arg_keys[1], (CYCLE, GROUP, CYCLE, PAIRS), 0, GROUP * NB), jax.random.fold_in(arg_keys[1], 1), 0, (GROUP * NB) - 1).astype(jnp.int32)
    pair_right = with_ends(jax.random.randint(arg_keys[2], (CYCLE, GROUP, CYCLE, PAIRS), 0, GROUP * NB), jax.random.fold_in(arg_keys[2], 1), 0, (GROUP * NB) - 1).astype(jnp.int32)
    pair_target = with_ends(jax.random.randint(arg_keys[3], (CYCLE, GROUP, CYCLE, PAIRS), 0, CS), jax.random.fold_in(arg_keys[3], 1), 0, CS - 1).astype(jnp.int32)
    return {"x_blocks": x_blocks, "pair_left": pair_left, "pair_right": pair_right, "pair_target": pair_target}


def member_terms(gathered, left_index, right_index, target_index):
    left_tiles = jnp.take(gathered, left_index, axis=0).astype(jnp.float32)
    right_tiles = jnp.take(gathered, right_index, axis=0).astype(jnp.float32)
    product = jnp.einsum("spxy,spxz->spyz", left_tiles, right_tiles, precision=lax.Precision.HIGHEST)
    selector = (target_index[:, :, None] == jnp.arange(CS, dtype=jnp.int32)[None, None, :]).astype(jnp.float32)
    return jnp.einsum("spc,spyz->scyz", selector, product, precision=lax.Precision.HIGHEST)


def reference(x_blocks, pair_left, pair_right, pair_target):
    span = GROUP * NB
    visit_ids = jnp.arange(CYCLE, dtype=jnp.int32)

    def visit(summed, group_id):
        gathered = lax.dynamic_slice_in_dim(x_blocks, (group_id * span).astype(jnp.int32), span, 0)
        left_index = lax.dynamic_index_in_dim(pair_left, group_id, 0, keepdims=False)
        right_index = lax.dynamic_index_in_dim(pair_right, group_id, 0, keepdims=False)
        target_index = lax.dynamic_index_in_dim(pair_target, group_id, 0, keepdims=False)

        def per_member(items):
            return member_terms(gathered, items[0], items[1], items[2])

        contrib = lax.map(per_member, (left_index, right_index, target_index))
        owners = ((group_id - 1 - visit_ids) % CYCLE).astype(jnp.int32)
        summed = summed.at[owners].add(jnp.swapaxes(contrib, 0, 1))
        return summed, None

    start_sum = jnp.zeros((CYCLE, GROUP, CS, BS, BS), jnp.float32)
    summed, _ = lax.scan(visit, start_sum, jnp.arange(CYCLE, dtype=jnp.int32))
    return summed.astype(jnp.bfloat16)
```

```python
import jax
import jax.numpy as jnp
from jax import lax
from jax.experimental import pallas as pl
from jax.experimental.pallas import tpu as pltpu
from jax.sharding import PartitionSpec as P

CS = 4
OWNERS_PER_STEP = 4


def _products_kernel(left_ref, right_ref, target_ref, x_ref, out_ref):
    step = pl.program_id(0)
    pair_count = left_ref.shape[0] // (pl.num_programs(0) * OWNERS_PER_STEP)
    out_ref[...] = jnp.zeros_like(out_ref)

    def body(j, carry):
        k = j // pair_count
        flat = step * OWNERS_PER_STEP * pair_count + j
        l = left_ref[flat]
        r = right_ref[flat]
        t = target_ref[flat]
        prod = lax.dot_general(
            x_ref[l], x_ref[r], (((0,), (0,)), ((), ())), preferred_element_type=jnp.float32
        )
        out_ref[k, t] += prod
        return carry

    lax.fori_loop(0, OWNERS_PER_STEP * pair_count, body, 0, unroll=4)


def owner_partials(gathered, left, right, target):
    owners, pair_count = left.shape
    block = gathered.shape[1]
    steps = owners // OWNERS_PER_STEP
    flops = 2 * owners * pair_count * block * block * block
    return pl.pallas_call(
        _products_kernel,
        out_shape=jax.ShapeDtypeStruct((owners, CS, block, block), jnp.float32),
        grid_spec=pltpu.PrefetchScalarGridSpec(
            num_scalar_prefetch=3,
            grid=(steps,),
            in_specs=[
                pl.BlockSpec(
                    gathered.shape,
                    lambda i, *_: (0, 0, 0),
                    pipeline_mode=pl.Buffered(1),
                )
            ],
            out_specs=pl.BlockSpec(
                (OWNERS_PER_STEP, CS, block, block), lambda i, *_: (i, 0, 0, 0)
            ),
        ),
        compiler_params=pltpu.CompilerParams(
            dimension_semantics=("arbitrary",), vmem_limit_bytes=48 * 1024 * 1024
        ),
        cost_estimate=pl.CostEstimate(
            flops=flops,
            transcendentals=0,
            bytes_accessed=gathered.size * 2 + owners * CS * block * block * 4,
        ),
    )(left.reshape(-1), right.reshape(-1), target.reshape(-1), gathered)


def per_device(x_blocks, pair_left, pair_right, pair_target):
    gathered = lax.all_gather(x_blocks, "grp", axis=0, tiled=True)
    group_count = lax.axis_size("blk")
    me = lax.axis_index("blk")
    visit = (me - 1 - jnp.arange(group_count, dtype=jnp.int32)) % group_count
    left = jnp.take(pair_left[0, 0], visit, axis=0)
    right = jnp.take(pair_right[0, 0], visit, axis=0)
    target = jnp.take(pair_target[0, 0], visit, axis=0)
    partials = owner_partials(gathered, left, right, target)
    summed = lax.psum_scatter(partials, "blk", scatter_dimension=0, tiled=True)
    block = x_blocks.shape[1]
    return summed.astype(jnp.bfloat16).reshape(1, 1, CS, block, block)


def solution(mesh):
    return jax.shard_map(
        per_device,
        mesh=mesh,
        in_specs=(
            P(("blk", "grp"), None, None),
            P("blk", "grp", None, None),
            P("blk", "grp", None, None),
            P("blk", "grp", None, None),
        ),
        out_specs=P("blk", "grp", None, None, None),
        check_vma=False,
    )
```

```python
import jax
import jax.numpy as jnp
from jax import lax
from jax.experimental import pallas as pl
from jax.experimental.pallas import tpu as pltpu
from jax.sharding import PartitionSpec as P

CS = 4
OWNERS_PER_STEP = 4


def _products_kernel(left_ref, right_ref, target_ref, x_ref, out_ref):
    step = pl.program_id(0)
    pair_count = left_ref.shape[0] // (pl.num_programs(0) * OWNERS_PER_STEP)
    out_ref[...] = jnp.zeros_like(out_ref)

    def body(j, carry):
        k = j // pair_count
        flat = step * OWNERS_PER_STEP * pair_count + j
        l = left_ref[flat]
        r = right_ref[flat]
        t = target_ref[flat]
        prod = lax.dot_general(
            x_ref[l], x_ref[r], (((0,), (0,)), ((), ())), preferred_element_type=jnp.float32
        )
        out_ref[t, k] += prod
        return carry

    lax.fori_loop(0, OWNERS_PER_STEP * pair_count, body, 0, unroll=4)


def owner_partials(gathered, left, right, target):
    owners, pair_count = left.shape
    block = gathered.shape[1]
    steps = owners // OWNERS_PER_STEP
    flops = 2 * owners * pair_count * block * block * block
    return pl.pallas_call(
        _products_kernel,
        out_shape=jax.ShapeDtypeStruct((CS, owners, block, block), jnp.float32),
        grid_spec=pltpu.PrefetchScalarGridSpec(
            num_scalar_prefetch=3,
            grid=(steps,),
            in_specs=[
                pl.BlockSpec(
                    gathered.shape,
                    lambda i, *_: (0, 0, 0),
                    pipeline_mode=pl.Buffered(1),
                )
            ],
            out_specs=pl.BlockSpec(
                (CS, OWNERS_PER_STEP, block, block), lambda i, *_: (0, i, 0, 0)
            ),
        ),
        compiler_params=pltpu.CompilerParams(
            dimension_semantics=("arbitrary",), vmem_limit_bytes=48 * 1024 * 1024
        ),
        cost_estimate=pl.CostEstimate(
            flops=flops,
            transcendentals=0,
            bytes_accessed=gathered.size * 2 + owners * CS * block * block * 4,
        ),
    )(left.reshape(-1), right.reshape(-1), target.reshape(-1), gathered)


BLK_DIMS = (4, 4, 2)


def _blk_coords(index):
    coords = []
    for size in reversed(BLK_DIMS):
        coords.append(index % size)
        index = index // size
    return tuple(reversed(coords))


def _blk_index(coords):
    index = 0
    for c, size in zip(coords, BLK_DIMS):
        index = index * size + c
    return index


def _shift_route(dim, step):
    route = []
    for b in range(_blk_index(tuple(s - 1 for s in BLK_DIMS)) + 1):
        coords = list(_blk_coords(b))
        coords[dim] = (coords[dim] + step) % BLK_DIMS[dim]
        route.append((b, _blk_index(tuple(coords))))
    return route


def ring_reduce_scatter(data, axis, dim, direction, coord):
    size = BLK_DIMS[dim]
    route = _shift_route(dim, direction)

    def piece(k):
        return lax.dynamic_index_in_dim(
            data, (coord - direction * (1 + k)) % size, axis, keepdims=False
        )

    send = piece(0)
    for k in range(size - 1):
        arrived = lax.ppermute(send, "blk", route)
        send = arrived + piece(k + 1)
    return send


def pair_reduce_scatter(data, dim, coord):
    route = _shift_route(dim, 1)
    other = lax.dynamic_index_in_dim(data, 1 - coord, 0, keepdims=False)
    mine = lax.dynamic_index_in_dim(data, coord, 0, keepdims=False)
    return lax.ppermute(other, "blk", route) + mine


def per_device(x_blocks, pair_left, pair_right, pair_target):
    gathered = lax.all_gather(x_blocks, "grp", axis=0, tiled=True)
    group_count = lax.axis_size("blk")
    assert group_count == BLK_DIMS[0] * BLK_DIMS[1] * BLK_DIMS[2]
    me = lax.axis_index("blk")
    visit = (me - 1 - jnp.arange(group_count, dtype=jnp.int32)) % group_count
    left = jnp.take(pair_left[0, 0], visit, axis=0)
    right = jnp.take(pair_right[0, 0], visit, axis=0)
    target = jnp.take(pair_target[0, 0], visit, axis=0)
    partials = owner_partials(gathered, left, right, target)
    block = x_blocks.shape[1]
    partials = partials.reshape((CS,) + BLK_DIMS + (block, block))
    my_y, my_x, my_z = _blk_coords(me)
    results = []
    for c in range(CS):
        data = partials[c]
        direction = 1 if c % 2 == 0 else -1
        if c < 2:
            data = ring_reduce_scatter(data, 1, 1, direction, my_x)
            data = ring_reduce_scatter(data, 0, 0, direction, my_y)
        else:
            data = ring_reduce_scatter(data, 0, 0, direction, my_y)
            data = ring_reduce_scatter(data, 0, 1, direction, my_x)
        results.append(pair_reduce_scatter(data, 2, my_z))
    summed = jnp.stack(results)
    return summed.astype(jnp.bfloat16).reshape(1, 1, CS, block, block)


def solution(mesh):
    return jax.shard_map(
        per_device,
        mesh=mesh,
        in_specs=(
            P(("blk", "grp"), None, None),
            P("blk", "grp", None, None),
            P("blk", "grp", None, None),
            P("blk", "grp", None, None),
        ),
        out_specs=P("blk", "grp", None, None, None),
        check_vma=False,
    )
```

```python
import jax
import jax.numpy as jnp
from jax import lax
from jax.experimental import pallas as pl
from jax.experimental.pallas import tpu as pltpu
from jax.sharding import PartitionSpec as P

CS = 4
OWNERS_PER_STEP = 4


def _products_kernel(left_ref, right_ref, target_ref, x_ref, out_ref):
    step = pl.program_id(0)
    pair_count = left_ref.shape[0] // (pl.num_programs(0) * OWNERS_PER_STEP)
    out_ref[...] = jnp.zeros_like(out_ref)

    def body(j, carry):
        k = j // pair_count
        flat = step * OWNERS_PER_STEP * pair_count + j
        l = left_ref[flat]
        r = right_ref[flat]
        t = target_ref[flat]
        prod = lax.dot_general(
            x_ref[l], x_ref[r], (((0,), (0,)), ((), ())), preferred_element_type=jnp.float32
        )
        out_ref[t, k] += prod
        return carry

    lax.fori_loop(0, OWNERS_PER_STEP * pair_count, body, 0, unroll=4)


def owner_partials(gathered, left, right, target):
    owners, pair_count = left.shape
    block = gathered.shape[1]
    steps = owners // OWNERS_PER_STEP
    flops = 2 * owners * pair_count * block * block * block
    return pl.pallas_call(
        _products_kernel,
        out_shape=jax.ShapeDtypeStruct((CS, owners, block, block), jnp.float32),
        grid_spec=pltpu.PrefetchScalarGridSpec(
            num_scalar_prefetch=3,
            grid=(steps,),
            in_specs=[
                pl.BlockSpec(
                    gathered.shape,
                    lambda i, *_: (0, 0, 0),
                    pipeline_mode=pl.Buffered(1),
                )
            ],
            out_specs=pl.BlockSpec(
                (CS, OWNERS_PER_STEP, block, block), lambda i, *_: (0, i, 0, 0)
            ),
        ),
        compiler_params=pltpu.CompilerParams(
            dimension_semantics=("arbitrary",), vmem_limit_bytes=48 * 1024 * 1024
        ),
        cost_estimate=pl.CostEstimate(
            flops=flops,
            transcendentals=0,
            bytes_accessed=gathered.size * 2 + owners * CS * block * block * 4,
        ),
    )(left.reshape(-1), right.reshape(-1), target.reshape(-1), gathered)


BLK_DIMS = (4, 4, 2)


def _blk_coords(index):
    coords = []
    for size in reversed(BLK_DIMS):
        coords.append(index % size)
        index = index // size
    return tuple(reversed(coords))


def _blk_index(coords):
    index = 0
    for c, size in zip(coords, BLK_DIMS):
        index = index * size + c
    return index


def _shift_route(dim, step, members):
    route = []
    for b in range(_blk_index(tuple(s - 1 for s in BLK_DIMS)) + 1):
        for g in range(members):
            coords = list(_blk_coords(b))
            move = step if g % 2 == 0 else -step
            coords[dim] = (coords[dim] + move) % BLK_DIMS[dim]
            route.append((b * members + g, _blk_index(tuple(coords)) * members + g))
    return route


def ring_reduce_scatter(data, axis, dim, direction, coord, members):
    size = BLK_DIMS[dim]
    route = _shift_route(dim, 1, members)

    def piece(k):
        return lax.dynamic_index_in_dim(
            data, (coord - direction * (1 + k)) % size, axis, keepdims=False
        )

    send = piece(0)
    for k in range(size - 1):
        arrived = lax.ppermute(send, ("blk", "grp"), route)
        send = arrived + piece(k + 1)
    return send


def pair_reduce_scatter(data, axis, dim, coord, members):
    route = _shift_route(dim, 1, members)
    other = lax.dynamic_index_in_dim(data, 1 - coord, axis, keepdims=False)
    mine = lax.dynamic_index_in_dim(data, coord, axis, keepdims=False)
    return lax.ppermute(other, ("blk", "grp"), route) + mine


def per_device(x_blocks, pair_left, pair_right, pair_target):
    gathered = lax.all_gather(x_blocks, "grp", axis=0, tiled=True)
    group_count = lax.axis_size("blk")
    members = lax.axis_size("grp")
    assert group_count == BLK_DIMS[0] * BLK_DIMS[1] * BLK_DIMS[2]
    me = lax.axis_index("blk")
    visit = (me - 1 - jnp.arange(group_count, dtype=jnp.int32)) % group_count
    left = jnp.take(pair_left[0, 0], visit, axis=0)
    right = jnp.take(pair_right[0, 0], visit, axis=0)
    target = jnp.take(pair_target[0, 0], visit, axis=0)
    partials = owner_partials(gathered, left, right, target)
    block = x_blocks.shape[1]
    partials = partials.reshape((CS,) + BLK_DIMS + (block, block))
    my_y, my_x, my_z = _blk_coords(me)
    direction = 1 - 2 * (lax.axis_index("grp") % 2)
    half = CS // 2
    first = ring_reduce_scatter(partials[:half], 2, 1, direction, my_x, members)
    first = ring_reduce_scatter(first, 1, 0, direction, my_y, members)
    second = ring_reduce_scatter(partials[half:], 1, 0, direction, my_y, members)
    second = ring_reduce_scatter(second, 1, 1, direction, my_x, members)
    both = jnp.concatenate([first, second], axis=0)
    summed = pair_reduce_scatter(both, 1, 2, my_z, members)
    return summed.astype(jnp.bfloat16).reshape(1, 1, CS, block, block)


def solution(mesh):
    return jax.shard_map(
        per_device,
        mesh=mesh,
        in_specs=(
            P(("blk", "grp"), None, None),
            P("blk", "grp", None, None),
            P("blk", "grp", None, None),
            P("blk", "grp", None, None),
        ),
        out_specs=P("blk", "grp", None, None, None),
        check_vma=False,
    )
```

```python
import jax
import jax.numpy as jnp
from jax import lax
from jax.experimental import pallas as pl
from jax.experimental.pallas import tpu as pltpu
from jax.sharding import PartitionSpec as P

CS = 4
OWNERS_PER_STEP = 4


def _products_kernel(left_ref, right_ref, target_ref, x_ref, *out_refs):
    step = pl.program_id(0)
    pair_count = left_ref.shape[0] // (pl.num_programs(0) * OWNERS_PER_STEP)
    for out_ref in out_refs:
        out_ref[...] = jnp.zeros_like(out_ref)

    def body(j, carry):
        k = j // pair_count
        flat = step * OWNERS_PER_STEP * pair_count + j
        l = left_ref[flat]
        r = right_ref[flat]
        t = target_ref[flat]
        prod = lax.dot_general(
            x_ref[l], x_ref[r], (((0,), (0,)), ((), ())), preferred_element_type=jnp.float32
        )
        for c, out_ref in enumerate(out_refs):

            @pl.when(t == c)
            def _(out_ref=out_ref):
                out_ref[k] += prod

        return carry

    lax.fori_loop(0, OWNERS_PER_STEP * pair_count, body, 0, unroll=4)


def owner_partials(gathered, left, right, target):
    owners, pair_count = left.shape
    block = gathered.shape[1]
    steps = owners // OWNERS_PER_STEP
    flops = 2 * owners * pair_count * block * block * block
    return pl.pallas_call(
        _products_kernel,
        out_shape=[jax.ShapeDtypeStruct((owners, block, block), jnp.float32)] * CS,
        grid_spec=pltpu.PrefetchScalarGridSpec(
            num_scalar_prefetch=3,
            grid=(steps,),
            in_specs=[
                pl.BlockSpec(
                    gathered.shape,
                    lambda i, *_: (0, 0, 0),
                    pipeline_mode=pl.Buffered(1),
                )
            ],
            out_specs=[
                pl.BlockSpec((OWNERS_PER_STEP, block, block), lambda i, *_: (i, 0, 0))
            ]
            * CS,
        ),
        compiler_params=pltpu.CompilerParams(
            dimension_semantics=("arbitrary",), vmem_limit_bytes=48 * 1024 * 1024
        ),
        cost_estimate=pl.CostEstimate(
            flops=flops,
            transcendentals=0,
            bytes_accessed=gathered.size * 2 + owners * CS * block * block * 4,
        ),
    )(left.reshape(-1), right.reshape(-1), target.reshape(-1), gathered)


BLK_DIMS = (4, 4, 2)


def _blk_coords(index):
    coords = []
    for size in reversed(BLK_DIMS):
        coords.append(index % size)
        index = index // size
    return tuple(reversed(coords))


def _blk_index(coords):
    index = 0
    for c, size in zip(coords, BLK_DIMS):
        index = index * size + c
    return index


def _shift_route(dim, step):
    route = []
    for b in range(_blk_index(tuple(s - 1 for s in BLK_DIMS)) + 1):
        coords = list(_blk_coords(b))
        coords[dim] = (coords[dim] + step) % BLK_DIMS[dim]
        route.append((b, _blk_index(tuple(coords))))
    return route


def ring_reduce_scatter(data, axis, dim, direction, coord):
    size = BLK_DIMS[dim]
    route = _shift_route(dim, direction)

    def piece(k):
        return lax.dynamic_index_in_dim(
            data, (coord - direction * (1 + k)) % size, axis, keepdims=False
        )

    send = piece(0)
    for k in range(size - 1):
        arrived = lax.ppermute(send, "blk", route)
        send = arrived + piece(k + 1)
    return send


def pair_reduce_scatter(data, dim, coord):
    route = _shift_route(dim, 1)
    other = lax.dynamic_index_in_dim(data, 1 - coord, 0, keepdims=False)
    mine = lax.dynamic_index_in_dim(data, coord, 0, keepdims=False)
    return lax.ppermute(other, "blk", route) + mine


LINE, CORES = 4, 2


def line_all_gather(own):
    z = lax.axis_index("grp") // CORES
    core = lax.axis_index("grp") % CORES
    members = LINE * CORES
    up = [(g, g + CORES) for g in range(members) if g // CORES < LINE - 1]
    down = [(g, g - CORES) for g in range(members) if g // CORES > 0]
    below, above = [], []
    send_up, send_down = own, own
    for _ in range(LINE - 1):
        send_up = lax.ppermute(send_up, "grp", up)
        send_down = lax.ppermute(send_down, "grp", down)
        below.append(send_up)
        above.append(send_down)
    below = jnp.stack(below)
    above = jnp.stack(above)
    mine = []
    for spot in range(LINE):
        from_below = lax.dynamic_index_in_dim(
            below, jnp.clip(z - 1 - spot, 0, LINE - 2), 0, keepdims=False
        )
        from_above = lax.dynamic_index_in_dim(
            above, jnp.clip(spot - z - 1, 0, LINE - 2), 0, keepdims=False
        )
        mine.append(
            jnp.where(spot == z, own, jnp.where(spot < z, from_below, from_above))
        )
    mine = jnp.stack(mine)
    sibling = [(g, g ^ 1) for g in range(members)]
    theirs = lax.ppermute(mine, "grp", sibling)
    first = jnp.where(core == 0, mine, theirs)
    second = jnp.where(core == 0, theirs, mine)
    gathered = jnp.stack([first, second], axis=1)
    return gathered.reshape((members * own.shape[0],) + own.shape[1:])


def per_device(x_blocks, pair_left, pair_right, pair_target):
    assert lax.axis_size("grp") == LINE * CORES
    gathered = line_all_gather(x_blocks)
    group_count = lax.axis_size("blk")
    assert group_count == BLK_DIMS[0] * BLK_DIMS[1] * BLK_DIMS[2]
    me = lax.axis_index("blk")
    visit = (me - 1 - jnp.arange(group_count, dtype=jnp.int32)) % group_count
    left = jnp.take(pair_left[0, 0], visit, axis=0)
    right = jnp.take(pair_right[0, 0], visit, axis=0)
    target = jnp.take(pair_target[0, 0], visit, axis=0)
    partials = owner_partials(gathered, left, right, target)
    block = x_blocks.shape[1]
    my_y, my_x, my_z = _blk_coords(me)
    results = []
    for c in range(CS):
        data = partials[c].reshape(BLK_DIMS + (block, block))
        direction = 1 if c % 2 == 0 else -1
        if c < 2:
            data = ring_reduce_scatter(data, 1, 1, direction, my_x)
            data = ring_reduce_scatter(data, 0, 0, direction, my_y)
        else:
            data = ring_reduce_scatter(data, 0, 0, direction, my_y)
            data = ring_reduce_scatter(data, 0, 1, direction, my_x)
        results.append(pair_reduce_scatter(data, 2, my_z))
    summed = jnp.stack(results)
    return summed.astype(jnp.bfloat16).reshape(1, 1, CS, block, block)


def solution(mesh):
    return jax.shard_map(
        per_device,
        mesh=mesh,
        in_specs=(
            P(("blk", "grp"), None, None),
            P("blk", "grp", None, None),
            P("blk", "grp", None, None),
            P("blk", "grp", None, None),
        ),
        out_specs=P("blk", "grp", None, None, None),
        check_vma=False,
    )
```

```python
import jax
import jax.numpy as jnp
from jax import lax
from jax.experimental import pallas as pl
from jax.experimental.pallas import tpu as pltpu
from jax.sharding import PartitionSpec as P

CS = 4
OWNERS_PER_STEP = 4


def _products_kernel(left_ref, right_ref, target_ref, x_ref, out_ref):
    step = pl.program_id(0)
    pair_count = left_ref.shape[0] // (pl.num_programs(0) * OWNERS_PER_STEP)
    out_ref[...] = jnp.zeros_like(out_ref)

    def body(j, carry):
        k = j // pair_count
        flat = step * OWNERS_PER_STEP * pair_count + j
        l = left_ref[flat]
        r = right_ref[flat]
        t = target_ref[flat]
        prod = lax.dot_general(
            x_ref[l], x_ref[r], (((0,), (0,)), ((), ())), preferred_element_type=jnp.float32
        )
        out_ref[t, k] += prod
        return carry

    lax.fori_loop(0, OWNERS_PER_STEP * pair_count, body, 0, unroll=4)


def owner_partials(gathered, left, right, target):
    owners, pair_count = left.shape
    block = gathered.shape[1]
    steps = owners // OWNERS_PER_STEP
    flops = 2 * owners * pair_count * block * block * block
    return pl.pallas_call(
        _products_kernel,
        out_shape=jax.ShapeDtypeStruct((CS, owners, block, block), jnp.float32),
        grid_spec=pltpu.PrefetchScalarGridSpec(
            num_scalar_prefetch=3,
            grid=(steps,),
            in_specs=[
                pl.BlockSpec(
                    gathered.shape,
                    lambda i, *_: (0, 0, 0),
                    pipeline_mode=pl.Buffered(1),
                )
            ],
            out_specs=pl.BlockSpec(
                (CS, OWNERS_PER_STEP, block, block), lambda i, *_: (0, i, 0, 0)
            ),
        ),
        compiler_params=pltpu.CompilerParams(
            dimension_semantics=("arbitrary",), vmem_limit_bytes=48 * 1024 * 1024
        ),
        cost_estimate=pl.CostEstimate(
            flops=flops,
            transcendentals=0,
            bytes_accessed=gathered.size * 2 + owners * CS * block * block * 4,
        ),
    )(left.reshape(-1), right.reshape(-1), target.reshape(-1), gathered)


BLK_DIMS = (4, 4, 2)


def _blk_coords(index):
    coords = []
    for size in reversed(BLK_DIMS):
        coords.append(index % size)
        index = index // size
    return tuple(reversed(coords))


def _blk_index(coords):
    index = 0
    for c, size in zip(coords, BLK_DIMS):
        index = index * size + c
    return index


def _shift_route(dim, step):
    route = []
    for b in range(_blk_index(tuple(s - 1 for s in BLK_DIMS)) + 1):
        coords = list(_blk_coords(b))
        coords[dim] = (coords[dim] + step) % BLK_DIMS[dim]
        route.append((b, _blk_index(tuple(coords))))
    return route


def _take(data, lead, axis, index):
    offset = len(lead)
    starts = [0] * data.ndim
    sizes = list(data.shape)
    for i, v in enumerate(lead):
        starts[i] = v
        sizes[i] = 1
    starts[offset + axis] = index
    sizes[offset + axis] = 1
    piece = lax.dynamic_slice(data, starts, sizes)
    return piece.reshape(
        [s for i, s in enumerate(sizes) if i >= offset and i != offset + axis]
    )


def ring_reduce_scatter(data, axis, dim, direction, coord, lead=()):
    size = BLK_DIMS[dim]
    route = _shift_route(dim, direction)

    def piece(k):
        return _take(data, lead, axis, (coord - direction * (1 + k)) % size)

    send = piece(0)
    for k in range(size - 1):
        arrived = lax.ppermute(send, "blk", route)
        send = arrived + piece(k + 1)
    return send


def pair_reduce_scatter(data, dim, coord):
    route = _shift_route(dim, 1)
    other = lax.dynamic_index_in_dim(data, 1 - coord, 0, keepdims=False)
    mine = lax.dynamic_index_in_dim(data, coord, 0, keepdims=False)
    return lax.ppermute(other, "blk", route) + mine


LINE, CORES = 4, 2


def line_all_gather(own):
    z = lax.axis_index("grp") // CORES
    core = lax.axis_index("grp") % CORES
    members = LINE * CORES
    up = [(g, g + CORES) for g in range(members) if g // CORES < LINE - 1]
    down = [(g, g - CORES) for g in range(members) if g // CORES > 0]
    below, above = [], []
    send_up, send_down = own, own
    for _ in range(LINE - 1):
        send_up = lax.ppermute(send_up, "grp", up)
        send_down = lax.ppermute(send_down, "grp", down)
        below.append(send_up)
        above.append(send_down)
    below = jnp.stack(below)
    above = jnp.stack(above)
    mine = []
    for spot in range(LINE):
        from_below = lax.dynamic_index_in_dim(
            below, jnp.clip(z - 1 - spot, 0, LINE - 2), 0, keepdims=False
        )
        from_above = lax.dynamic_index_in_dim(
            above, jnp.clip(spot - z - 1, 0, LINE - 2), 0, keepdims=False
        )
        mine.append(
            jnp.where(spot == z, own, jnp.where(spot < z, from_below, from_above))
        )
    mine = jnp.stack(mine)
    sibling = [(g, g ^ 1) for g in range(members)]
    theirs = lax.ppermute(mine, "grp", sibling)
    first = jnp.where(core == 0, mine, theirs)
    second = jnp.where(core == 0, theirs, mine)
    gathered = jnp.stack([first, second], axis=1)
    return gathered.reshape((members * own.shape[0],) + own.shape[1:])


def per_device(x_blocks, pair_left, pair_right, pair_target):
    assert lax.axis_size("grp") == LINE * CORES
    gathered = line_all_gather(x_blocks)
    group_count = lax.axis_size("blk")
    assert group_count == BLK_DIMS[0] * BLK_DIMS[1] * BLK_DIMS[2]
    me = lax.axis_index("blk")
    visit = (me - 1 - jnp.arange(group_count, dtype=jnp.int32)) % group_count
    left = jnp.take(pair_left[0, 0], visit, axis=0)
    right = jnp.take(pair_right[0, 0], visit, axis=0)
    target = jnp.take(pair_target[0, 0], visit, axis=0)
    partials = owner_partials(gathered, left, right, target)
    block = x_blocks.shape[1]
    my_y, my_x, my_z = _blk_coords(me)
    partials = partials.reshape((CS,) + BLK_DIMS + (block, block))
    results = []
    for c in range(CS):
        direction = 1 if c % 2 == 0 else -1
        if c < 2:
            data = ring_reduce_scatter(partials, 1, 1, direction, my_x, (c,))
            data = ring_reduce_scatter(data, 0, 0, direction, my_y)
        else:
            data = ring_reduce_scatter(partials, 0, 0, direction, my_y, (c,))
            data = ring_reduce_scatter(data, 0, 1, direction, my_x)
        results.append(pair_reduce_scatter(data, 2, my_z))
    summed = jnp.stack(results)
    return summed.astype(jnp.bfloat16).reshape(1, 1, CS, block, block)


def solution(mesh):
    return jax.shard_map(
        per_device,
        mesh=mesh,
        in_specs=(
            P(("blk", "grp"), None, None),
            P("blk", "grp", None, None),
            P("blk", "grp", None, None),
            P("blk", "grp", None, None),
        ),
        out_specs=P("blk", "grp", None, None, None),
        check_vma=False,
    )
```

```python
import jax
import jax.numpy as jnp
from jax import lax
from jax.experimental import pallas as pl
from jax.experimental.pallas import tpu as pltpu
from jax.sharding import PartitionSpec as P

CS = 4
OWNERS_PER_STEP = 4


def _products_kernel(left_ref, right_ref, target_ref, x_ref, out_ref):
    step = pl.program_id(0)
    pair_count = left_ref.shape[0] // (pl.num_programs(0) * OWNERS_PER_STEP)
    out_ref[...] = jnp.zeros_like(out_ref)

    def body(j, carry):
        k = j // pair_count
        flat = step * OWNERS_PER_STEP * pair_count + j
        l = left_ref[flat]
        r = right_ref[flat]
        t = target_ref[flat]
        prod = lax.dot_general(
            x_ref[l], x_ref[r], (((0,), (0,)), ((), ())), preferred_element_type=jnp.float32
        )
        out_ref[t, k] += prod
        return carry

    lax.fori_loop(0, OWNERS_PER_STEP * pair_count, body, 0, unroll=4)


def owner_partials(gathered, left, right, target):
    owners, pair_count = left.shape
    block = gathered.shape[1]
    steps = owners // OWNERS_PER_STEP
    flops = 2 * owners * pair_count * block * block * block
    return pl.pallas_call(
        _products_kernel,
        out_shape=jax.ShapeDtypeStruct((CS, owners, block, block), jnp.float32),
        grid_spec=pltpu.PrefetchScalarGridSpec(
            num_scalar_prefetch=3,
            grid=(steps,),
            in_specs=[
                pl.BlockSpec(
                    gathered.shape,
                    lambda i, *_: (0, 0, 0),
                    pipeline_mode=pl.Buffered(1),
                )
            ],
            out_specs=pl.BlockSpec(
                (CS, OWNERS_PER_STEP, block, block), lambda i, *_: (0, i, 0, 0)
            ),
        ),
        compiler_params=pltpu.CompilerParams(
            dimension_semantics=("arbitrary",), vmem_limit_bytes=48 * 1024 * 1024
        ),
        cost_estimate=pl.CostEstimate(
            flops=flops,
            transcendentals=0,
            bytes_accessed=gathered.size * 2 + owners * CS * block * block * 4,
        ),
    )(left.reshape(-1), right.reshape(-1), target.reshape(-1), gathered)


BLK_DIMS = (4, 4, 2)


def _blk_coords(index):
    coords = []
    for size in reversed(BLK_DIMS):
        coords.append(index % size)
        index = index // size
    return tuple(reversed(coords))


def _blk_index(coords):
    index = 0
    for c, size in zip(coords, BLK_DIMS):
        index = index * size + c
    return index


def _shift_route(dim, step):
    route = []
    for b in range(_blk_index(tuple(s - 1 for s in BLK_DIMS)) + 1):
        coords = list(_blk_coords(b))
        coords[dim] = (coords[dim] + step) % BLK_DIMS[dim]
        route.append((b, _blk_index(tuple(coords))))
    return route


def _take(data, lead, axis, index):
    offset = len(lead)
    starts = [0] * data.ndim
    sizes = list(data.shape)
    for i, v in enumerate(lead):
        starts[i] = v
        sizes[i] = 1
    starts[offset + axis] = index
    sizes[offset + axis] = 1
    piece = lax.dynamic_slice(data, starts, sizes)
    return piece.reshape(
        [s for i, s in enumerate(sizes) if i >= offset and i != offset + axis]
    )


def ring_reduce_scatter(data, axis, dim, direction, coord, lead=()):
    size = BLK_DIMS[dim]
    route = _shift_route(dim, direction)

    def piece(k):
        return _take(data, lead, axis, (coord - direction * (1 + k)) % size)

    send = piece(0)
    for k in range(size - 1):
        arrived = lax.ppermute(send, "blk", route)
        send = arrived + piece(k + 1)
    return send


def pair_reduce_scatter(data, dim, coord):
    route = _shift_route(dim, 1)
    other = lax.dynamic_index_in_dim(data, 1 - coord, 0, keepdims=False)
    mine = lax.dynamic_index_in_dim(data, coord, 0, keepdims=False)
    return lax.ppermute(other, "blk", route) + mine


LINE, CORES = 4, 2


def line_all_gather(own):
    z = lax.axis_index("grp") // CORES
    core = lax.axis_index("grp") % CORES
    members = LINE * CORES
    up = [(g, g + CORES) for g in range(members) if g // CORES < LINE - 1]
    down = [(g, g - CORES) for g in range(members) if g // CORES > 0]
    below, above = [], []
    send_up, send_down = own, own
    for _ in range(LINE - 1):
        send_up = lax.ppermute(send_up, "grp", up)
        send_down = lax.ppermute(send_down, "grp", down)
        below.append(send_up)
        above.append(send_down)
    below = jnp.stack(below)
    above = jnp.stack(above)
    mine = []
    for spot in range(LINE):
        from_below = lax.dynamic_index_in_dim(
            below, jnp.clip(z - 1 - spot, 0, LINE - 2), 0, keepdims=False
        )
        from_above = lax.dynamic_index_in_dim(
            above, jnp.clip(spot - z - 1, 0, LINE - 2), 0, keepdims=False
        )
        mine.append(
            jnp.where(spot == z, own, jnp.where(spot < z, from_below, from_above))
        )
    mine = jnp.stack(mine)
    sibling = [(g, g ^ 1) for g in range(members)]
    theirs = lax.ppermute(mine, "grp", sibling)
    first = jnp.where(core == 0, mine, theirs)
    second = jnp.where(core == 0, theirs, mine)
    gathered = jnp.stack([first, second], axis=1)
    return gathered.reshape((members * own.shape[0],) + own.shape[1:])


def per_device(x_blocks, pair_left, pair_right, pair_target):
    assert lax.axis_size("grp") == LINE * CORES
    gathered = line_all_gather(x_blocks)
    group_count = lax.axis_size("blk")
    assert group_count == BLK_DIMS[0] * BLK_DIMS[1] * BLK_DIMS[2]
    me = lax.axis_index("blk")
    visit = (me - 1 - jnp.arange(group_count, dtype=jnp.int32)) % group_count
    left = jnp.take(pair_left[0, 0], visit, axis=0)
    right = jnp.take(pair_right[0, 0], visit, axis=0)
    target = jnp.take(pair_target[0, 0], visit, axis=0)
    partials = owner_partials(gathered, left, right, target)
    block = x_blocks.shape[1]
    my_y, my_x, my_z = _blk_coords(me)
    partials = partials.reshape((CS,) + BLK_DIMS + (block, block))
    results = []
    for c in range(CS):
        data = partials[c]
        direction = 1 if c % 2 == 0 else -1
        if c < 2:
            data = ring_reduce_scatter(data, 1, 1, direction, my_x)
            data = ring_reduce_scatter(data, 0, 0, direction, my_y)
        else:
            data = ring_reduce_scatter(data, 0, 0, direction, my_y)
            data = ring_reduce_scatter(data, 0, 1, direction, my_x)
        results.append(pair_reduce_scatter(data, 2, my_z))
    summed = jnp.stack(results)
    return summed.astype(jnp.bfloat16).reshape(1, 1, CS, block, block)


def solution(mesh):
    return jax.shard_map(
        per_device,
        mesh=mesh,
        in_specs=(
            P(("blk", "grp"), None, None),
            P("blk", "grp", None, None),
            P("blk", "grp", None, None),
            P("blk", "grp", None, None),
        ),
        out_specs=P("blk", "grp", None, None, None),
        check_vma=False,
    )
```

```python
import jax
import jax.numpy as jnp
from jax import lax
from jax.experimental import pallas as pl
from jax.experimental.pallas import tpu as pltpu
from jax.sharding import PartitionSpec as P

CS = 4
OWNERS_PER_STEP = 4


def _products_kernel(left_ref, right_ref, target_ref, x_ref, *refs):
    out_refs, acc_ref = refs[:CS], refs[CS]
    step = pl.program_id(0)
    pair_count = left_ref.shape[0] // (pl.num_programs(0) * OWNERS_PER_STEP)
    acc_ref[...] = jnp.zeros_like(acc_ref)

    def body(j, carry):
        k = j // pair_count
        flat = step * OWNERS_PER_STEP * pair_count + j
        l = left_ref[flat]
        r = right_ref[flat]
        t = target_ref[flat]
        prod = lax.dot_general(
            x_ref[l], x_ref[r], (((0,), (0,)), ((), ())), preferred_element_type=jnp.float32
        )
        acc_ref[t, k] += prod
        return carry

    lax.fori_loop(0, OWNERS_PER_STEP * pair_count, body, 0, unroll=4)
    for c, out_ref in enumerate(out_refs):
        out_ref[...] = acc_ref[c]


def owner_partials(gathered, left, right, target):
    owners, pair_count = left.shape
    block = gathered.shape[1]
    steps = owners // OWNERS_PER_STEP
    flops = 2 * owners * pair_count * block * block * block
    return pl.pallas_call(
        _products_kernel,
        out_shape=[jax.ShapeDtypeStruct((owners, block, block), jnp.float32)] * CS,
        grid_spec=pltpu.PrefetchScalarGridSpec(
            num_scalar_prefetch=3,
            grid=(steps,),
            in_specs=[
                pl.BlockSpec(
                    gathered.shape,
                    lambda i, *_: (0, 0, 0),
                    pipeline_mode=pl.Buffered(1),
                )
            ],
            out_specs=[
                pl.BlockSpec((OWNERS_PER_STEP, block, block), lambda i, *_: (i, 0, 0))
            ]
            * CS,
            scratch_shapes=[pltpu.VMEM((CS, OWNERS_PER_STEP, block, block), jnp.float32)],
        ),
        compiler_params=pltpu.CompilerParams(
            dimension_semantics=("arbitrary",), vmem_limit_bytes=48 * 1024 * 1024
        ),
        cost_estimate=pl.CostEstimate(
            flops=flops,
            transcendentals=0,
            bytes_accessed=gathered.size * 2 + owners * CS * block * block * 4,
        ),
    )(left.reshape(-1), right.reshape(-1), target.reshape(-1), gathered)


BLK_DIMS = (4, 4, 2)


def _blk_coords(index):
    coords = []
    for size in reversed(BLK_DIMS):
        coords.append(index % size)
        index = index // size
    return tuple(reversed(coords))


def _blk_index(coords):
    index = 0
    for c, size in zip(coords, BLK_DIMS):
        index = index * size + c
    return index


def _shift_route(dim, step):
    route = []
    for b in range(_blk_index(tuple(s - 1 for s in BLK_DIMS)) + 1):
        coords = list(_blk_coords(b))
        coords[dim] = (coords[dim] + step) % BLK_DIMS[dim]
        route.append((b, _blk_index(tuple(coords))))
    return route


def _take(data, lead, axis, index):
    offset = len(lead)
    starts = [0] * data.ndim
    sizes = list(data.shape)
    for i, v in enumerate(lead):
        starts[i] = v
        sizes[i] = 1
    starts[offset + axis] = index
    sizes[offset + axis] = 1
    piece = lax.dynamic_slice(data, starts, sizes)
    return piece.reshape(
        [s for i, s in enumerate(sizes) if i >= offset and i != offset + axis]
    )


def ring_reduce_scatter(data, axis, dim, direction, coord, lead=()):
    size = BLK_DIMS[dim]
    route = _shift_route(dim, direction)

    def piece(k):
        return _take(data, lead, axis, (coord - direction * (1 + k)) % size)

    send = piece(0)
    for k in range(size - 1):
        arrived = lax.ppermute(send, "blk", route)
        send = arrived + piece(k + 1)
    return send


def pair_reduce_scatter(data, axis, coord):
    route = _shift_route(2, 1)
    other = lax.dynamic_index_in_dim(data, 1 - coord, axis, keepdims=False)
    mine = lax.dynamic_index_in_dim(data, coord, axis, keepdims=False)
    return lax.ppermute(other, "blk", route) + mine


LINE, CORES = 4, 2


def line_all_gather(own):
    z = lax.axis_index("grp") // CORES
    core = lax.axis_index("grp") % CORES
    members = LINE * CORES
    up = [(g, g + CORES) for g in range(members) if g // CORES < LINE - 1]
    down = [(g, g - CORES) for g in range(members) if g // CORES > 0]
    below, above = [], []
    send_up, send_down = own, own
    for _ in range(LINE - 1):
        send_up = lax.ppermute(send_up, "grp", up)
        send_down = lax.ppermute(send_down, "grp", down)
        below.append(send_up)
        above.append(send_down)
    below = jnp.stack(below)
    above = jnp.stack(above)
    mine = []
    for spot in range(LINE):
        from_below = lax.dynamic_index_in_dim(
            below, jnp.clip(z - 1 - spot, 0, LINE - 2), 0, keepdims=False
        )
        from_above = lax.dynamic_index_in_dim(
            above, jnp.clip(spot - z - 1, 0, LINE - 2), 0, keepdims=False
        )
        mine.append(
            jnp.where(spot == z, own, jnp.where(spot < z, from_below, from_above))
        )
    mine = jnp.stack(mine)
    sibling = [(g, g ^ 1) for g in range(members)]
    theirs = lax.ppermute(mine, "grp", sibling)
    first = jnp.where(core == 0, mine, theirs)
    second = jnp.where(core == 0, theirs, mine)
    gathered = jnp.stack([first, second], axis=1)
    return gathered.reshape((members * own.shape[0],) + own.shape[1:])


def per_device(x_blocks, pair_left, pair_right, pair_target):
    assert lax.axis_size("grp") == LINE * CORES
    gathered = line_all_gather(x_blocks)
    group_count = lax.axis_size("blk")
    assert group_count == BLK_DIMS[0] * BLK_DIMS[1] * BLK_DIMS[2]
    me = lax.axis_index("blk")
    visit = (me - 1 - jnp.arange(group_count, dtype=jnp.int32)) % group_count
    left = jnp.take(pair_left[0, 0], visit, axis=0)
    right = jnp.take(pair_right[0, 0], visit, axis=0)
    target = jnp.take(pair_target[0, 0], visit, axis=0)
    partials = owner_partials(gathered, left, right, target)
    block = x_blocks.shape[1]
    my_y, my_x, my_z = _blk_coords(me)
    results = []
    for c in range(CS):
        data = partials[c].reshape(BLK_DIMS + (block, block))
        direction = 1 if c % 2 == 0 else -1
        if c < 2:
            data = ring_reduce_scatter(data, 1, 1, direction, my_x)
            data = ring_reduce_scatter(data, 0, 0, direction, my_y)
        else:
            data = ring_reduce_scatter(data, 0, 0, direction, my_y)
            data = ring_reduce_scatter(data, 0, 1, direction, my_x)
        results.append(data)
    summed = pair_reduce_scatter(jnp.stack(results), 1, my_z)
    return summed.astype(jnp.bfloat16).reshape(1, 1, CS, block, block)


def solution(mesh):
    return jax.shard_map(
        per_device,
        mesh=mesh,
        in_specs=(
            P(("blk", "grp"), None, None),
            P("blk", "grp", None, None),
            P("blk", "grp", None, None),
            P("blk", "grp", None, None),
        ),
        out_specs=P("blk", "grp", None, None, None),
        check_vma=False,
    )
```

```python
import jax
import jax.numpy as jnp
from jax import lax
from jax.experimental import pallas as pl
from jax.experimental.pallas import tpu as pltpu
from jax.sharding import PartitionSpec as P

CS = 4
OWNERS_PER_STEP = 4


def _products_kernel(left_ref, right_ref, target_ref, x_ref, *refs):
    out_refs, acc_ref = refs[:CS], refs[CS]
    step = pl.program_id(0)
    pair_count = left_ref.shape[0] // (pl.num_programs(0) * OWNERS_PER_STEP)
    acc_ref[...] = jnp.zeros_like(acc_ref)

    def body(j, carry):
        k = j // pair_count
        flat = step * OWNERS_PER_STEP * pair_count + j
        l = left_ref[flat]
        r = right_ref[flat]
        t = target_ref[flat]
        prod = lax.dot_general(
            x_ref[l], x_ref[r], (((0,), (0,)), ((), ())), preferred_element_type=jnp.float32
        )
        acc_ref[t, k] += prod
        return carry

    lax.fori_loop(0, OWNERS_PER_STEP * pair_count, body, 0, unroll=4)
    for c, out_ref in enumerate(out_refs):
        out_ref[...] = acc_ref[c]


def owner_partials(gathered, left, right, target):
    owners, pair_count = left.shape
    block = gathered.shape[1]
    steps = owners // OWNERS_PER_STEP
    flops = 2 * owners * pair_count * block * block * block
    return pl.pallas_call(
        _products_kernel,
        out_shape=[jax.ShapeDtypeStruct((owners, block, block), jnp.float32)] * CS,
        grid_spec=pltpu.PrefetchScalarGridSpec(
            num_scalar_prefetch=3,
            grid=(steps,),
            in_specs=[
                pl.BlockSpec(
                    gathered.shape,
                    lambda i, *_: (0, 0, 0),
                    pipeline_mode=pl.Buffered(1),
                )
            ],
            out_specs=[
                pl.BlockSpec((OWNERS_PER_STEP, block, block), lambda i, *_: (i, 0, 0))
            ]
            * CS,
            scratch_shapes=[pltpu.VMEM((CS, OWNERS_PER_STEP, block, block), jnp.float32)],
        ),
        compiler_params=pltpu.CompilerParams(
            dimension_semantics=("arbitrary",), vmem_limit_bytes=48 * 1024 * 1024
        ),
        cost_estimate=pl.CostEstimate(
            flops=flops,
            transcendentals=0,
            bytes_accessed=gathered.size * 2 + owners * CS * block * block * 4,
        ),
    )(left.reshape(-1), right.reshape(-1), target.reshape(-1), gathered)


BLK_DIMS = (4, 4, 2)


def _blk_coords(index):
    coords = []
    for size in reversed(BLK_DIMS):
        coords.append(index % size)
        index = index // size
    return tuple(reversed(coords))


def _blk_index(coords):
    index = 0
    for c, size in zip(coords, BLK_DIMS):
        index = index * size + c
    return index


def _shift_route(dim, step):
    route = []
    for b in range(_blk_index(tuple(s - 1 for s in BLK_DIMS)) + 1):
        coords = list(_blk_coords(b))
        coords[dim] = (coords[dim] + step) % BLK_DIMS[dim]
        route.append((b, _blk_index(tuple(coords))))
    return route


def _take(data, lead, axis, index):
    offset = len(lead)
    starts = [0] * data.ndim
    sizes = list(data.shape)
    for i, v in enumerate(lead):
        starts[i] = v
        sizes[i] = 1
    starts[offset + axis] = index
    sizes[offset + axis] = 1
    piece = lax.dynamic_slice(data, starts, sizes)
    return piece.reshape(
        [s for i, s in enumerate(sizes) if i >= offset and i != offset + axis]
    )


def ring_reduce_scatter(data, axis, dim, direction, coord, lead=()):
    size = BLK_DIMS[dim]
    route = _shift_route(dim, direction)

    def piece(k):
        return _take(data, lead, axis, (coord - direction * (1 + k)) % size)

    send = piece(0)
    for k in range(size - 1):
        arrived = lax.ppermute(send, "blk", route)
        send = arrived + piece(k + 1)
    return send


def pair_reduce_scatter(data, axis, coord):
    route = _shift_route(2, 1)
    other = lax.dynamic_index_in_dim(data, 1 - coord, axis, keepdims=False)
    mine = lax.dynamic_index_in_dim(data, coord, axis, keepdims=False)
    return lax.ppermute(other, "blk", route) + mine


LINE, CORES = 4, 2


def line_all_gather(own):
    z = lax.axis_index("grp") // CORES
    core = lax.axis_index("grp") % CORES
    members = LINE * CORES
    up = [(g, g + CORES) for g in range(members) if g // CORES < LINE - 1]
    down = [(g, g - CORES) for g in range(members) if g // CORES > 0]
    below, above = [], []
    send_up, send_down = own, own
    for _ in range(LINE - 1):
        send_up = lax.ppermute(send_up, "grp", up)
        send_down = lax.ppermute(send_down, "grp", down)
        below.append(send_up)
        above.append(send_down)
    below = jnp.stack(below)
    above = jnp.stack(above)
    mine = []
    for spot in range(LINE):
        from_below = lax.dynamic_index_in_dim(
            below, jnp.clip(z - 1 - spot, 0, LINE - 2), 0, keepdims=False
        )
        from_above = lax.dynamic_index_in_dim(
            above, jnp.clip(spot - z - 1, 0, LINE - 2), 0, keepdims=False
        )
        mine.append(
            jnp.where(spot == z, own, jnp.where(spot < z, from_below, from_above))
        )
    mine = jnp.stack(mine)
    sibling = [(g, g ^ 1) for g in range(members)]
    theirs = lax.ppermute(mine, "grp", sibling)
    first = jnp.where(core == 0, mine, theirs)
    second = jnp.where(core == 0, theirs, mine)
    gathered = jnp.stack([first, second], axis=1)
    return gathered.reshape((members * own.shape[0],) + own.shape[1:])


def per_device(x_blocks, pair_left, pair_right, pair_target):
    assert lax.axis_size("grp") == LINE * CORES
    gathered = line_all_gather(x_blocks)
    group_count = lax.axis_size("blk")
    assert group_count == BLK_DIMS[0] * BLK_DIMS[1] * BLK_DIMS[2]
    me = lax.axis_index("blk")
    visit = (me - 1 - jnp.arange(group_count, dtype=jnp.int32)) % group_count
    left = jnp.take(pair_left[0, 0], visit, axis=0)
    right = jnp.take(pair_right[0, 0], visit, axis=0)
    target = jnp.take(pair_target[0, 0], visit, axis=0)
    partials = owner_partials(gathered, left, right, target)
    block = x_blocks.shape[1]
    my_y, my_x, my_z = _blk_coords(me)
    firsts = []
    for c in range(CS):
        data = partials[c].reshape(BLK_DIMS + (block, block))
        direction = 1 if c % 2 == 0 else -1
        if c < 2:
            firsts.append(ring_reduce_scatter(data, 1, 1, direction, my_x))
        else:
            firsts.append(ring_reduce_scatter(data, 0, 0, direction, my_y))
    half = CS // 2
    along_y = ring_reduce_scatter(jnp.stack(firsts[:half]), 1, 0, 1, my_y)
    along_x = ring_reduce_scatter(jnp.stack(firsts[half:]), 1, 1, 1, my_x)
    results = jnp.concatenate([along_y, along_x])
    summed = pair_reduce_scatter(results, 1, my_z)
    return summed.astype(jnp.bfloat16).reshape(1, 1, CS, block, block)


def solution(mesh):
    return jax.shard_map(
        per_device,
        mesh=mesh,
        in_specs=(
            P(("blk", "grp"), None, None),
            P("blk", "grp", None, None),
            P("blk", "grp", None, None),
            P("blk", "grp", None, None),
        ),
        out_specs=P("blk", "grp", None, None, None),
        check_vma=False,
    )
```

```python
import jax
import jax.numpy as jnp
from jax import lax
from jax.experimental import pallas as pl
from jax.experimental.pallas import tpu as pltpu
from jax.sharding import PartitionSpec as P

CS = 4
OWNERS_PER_STEP = 4


def _products_kernel(left_ref, right_ref, target_ref, x_ref, *refs):
    out_refs, acc_ref = refs[:CS], refs[CS]
    step = pl.program_id(0)
    pair_count = left_ref.shape[0] // (pl.num_programs(0) * OWNERS_PER_STEP)
    acc_ref[...] = jnp.zeros_like(acc_ref)

    def body(j, carry):
        k = j // pair_count
        flat = step * OWNERS_PER_STEP * pair_count + j
        l = left_ref[flat]
        r = right_ref[flat]
        t = target_ref[flat]
        prod = lax.dot_general(
            x_ref[l], x_ref[r], (((0,), (0,)), ((), ())), preferred_element_type=jnp.float32
        )
        acc_ref[t, k] += prod
        return carry

    lax.fori_loop(0, OWNERS_PER_STEP * pair_count, body, 0, unroll=4)
    for c, out_ref in enumerate(out_refs):
        out_ref[...] = acc_ref[c]


def owner_partials(gathered, left, right, target):
    owners, pair_count = left.shape
    block = gathered.shape[1]
    steps = owners // OWNERS_PER_STEP
    flops = 2 * owners * pair_count * block * block * block
    return pl.pallas_call(
        _products_kernel,
        out_shape=[jax.ShapeDtypeStruct((owners, block, block), jnp.float32)] * CS,
        grid_spec=pltpu.PrefetchScalarGridSpec(
            num_scalar_prefetch=3,
            grid=(steps,),
            in_specs=[
                pl.BlockSpec(
                    gathered.shape,
                    lambda i, *_: (0, 0, 0),
                    pipeline_mode=pl.Buffered(1),
                )
            ],
            out_specs=[
                pl.BlockSpec((OWNERS_PER_STEP, block, block), lambda i, *_: (i, 0, 0))
            ]
            * CS,
            scratch_shapes=[pltpu.VMEM((CS, OWNERS_PER_STEP, block, block), jnp.float32)],
        ),
        compiler_params=pltpu.CompilerParams(
            dimension_semantics=("arbitrary",), vmem_limit_bytes=48 * 1024 * 1024
        ),
        cost_estimate=pl.CostEstimate(
            flops=flops,
            transcendentals=0,
            bytes_accessed=gathered.size * 2 + owners * CS * block * block * 4,
        ),
    )(left.reshape(-1), right.reshape(-1), target.reshape(-1), gathered)


BLK_DIMS = (4, 4, 2)


def _blk_coords(index):
    coords = []
    for size in reversed(BLK_DIMS):
        coords.append(index % size)
        index = index // size
    return tuple(reversed(coords))


def _blk_index(coords):
    index = 0
    for c, size in zip(coords, BLK_DIMS):
        index = index * size + c
    return index


def _shift_route(dim, step):
    route = []
    for b in range(_blk_index(tuple(s - 1 for s in BLK_DIMS)) + 1):
        coords = list(_blk_coords(b))
        coords[dim] = (coords[dim] + step) % BLK_DIMS[dim]
        route.append((b, _blk_index(tuple(coords))))
    return route


def _take(data, lead, axis, index):
    offset = len(lead)
    starts = [0] * data.ndim
    sizes = list(data.shape)
    for i, v in enumerate(lead):
        starts[i] = v
        sizes[i] = 1
    starts[offset + axis] = index
    sizes[offset + axis] = 1
    piece = lax.dynamic_slice(data, starts, sizes)
    return piece.reshape(
        [s for i, s in enumerate(sizes) if i >= offset and i != offset + axis]
    )


def ring_reduce_scatter(data, axis, dim, direction, coord, lead=()):
    size = BLK_DIMS[dim]
    route = _shift_route(dim, direction)

    def piece(k):
        return _take(data, lead, axis, (coord - direction * (1 + k)) % size)

    send = piece(0)
    for k in range(size - 1):
        arrived = lax.ppermute(send, "blk", route)
        send = arrived + piece(k + 1)
    return send


def direct_reduce_scatter(data, axis, dim, coord):
    size = BLK_DIMS[dim]
    total = lax.dynamic_index_in_dim(data, coord, axis, keepdims=False)
    for shift in range(1, size):
        piece = lax.dynamic_index_in_dim(data, (coord + shift) % size, axis, keepdims=False)
        total = total + lax.ppermute(piece, "blk", _shift_route(dim, shift))
    return total


def pair_reduce_scatter(data, axis, coord):
    route = _shift_route(2, 1)
    other = lax.dynamic_index_in_dim(data, 1 - coord, axis, keepdims=False)
    mine = lax.dynamic_index_in_dim(data, coord, axis, keepdims=False)
    return lax.ppermute(other, "blk", route) + mine


LINE, CORES = 4, 2


def line_all_gather(own):
    z = lax.axis_index("grp") // CORES
    core = lax.axis_index("grp") % CORES
    members = LINE * CORES
    up = [(g, g + CORES) for g in range(members) if g // CORES < LINE - 1]
    down = [(g, g - CORES) for g in range(members) if g // CORES > 0]
    below, above = [], []
    send_up, send_down = own, own
    for _ in range(LINE - 1):
        send_up = lax.ppermute(send_up, "grp", up)
        send_down = lax.ppermute(send_down, "grp", down)
        below.append(send_up)
        above.append(send_down)
    below = jnp.stack(below)
    above = jnp.stack(above)
    mine = []
    for spot in range(LINE):
        from_below = lax.dynamic_index_in_dim(
            below, jnp.clip(z - 1 - spot, 0, LINE - 2), 0, keepdims=False
        )
        from_above = lax.dynamic_index_in_dim(
            above, jnp.clip(spot - z - 1, 0, LINE - 2), 0, keepdims=False
        )
        mine.append(
            jnp.where(spot == z, own, jnp.where(spot < z, from_below, from_above))
        )
    mine = jnp.stack(mine)
    sibling = [(g, g ^ 1) for g in range(members)]
    theirs = lax.ppermute(mine, "grp", sibling)
    first = jnp.where(core == 0, mine, theirs)
    second = jnp.where(core == 0, theirs, mine)
    gathered = jnp.stack([first, second], axis=1)
    return gathered.reshape((members * own.shape[0],) + own.shape[1:])


def per_device(x_blocks, pair_left, pair_right, pair_target):
    assert lax.axis_size("grp") == LINE * CORES
    gathered = line_all_gather(x_blocks)
    group_count = lax.axis_size("blk")
    assert group_count == BLK_DIMS[0] * BLK_DIMS[1] * BLK_DIMS[2]
    me = lax.axis_index("blk")
    visit = (me - 1 - jnp.arange(group_count, dtype=jnp.int32)) % group_count
    left = jnp.take(pair_left[0, 0], visit, axis=0)
    right = jnp.take(pair_right[0, 0], visit, axis=0)
    target = jnp.take(pair_target[0, 0], visit, axis=0)
    partials = owner_partials(gathered, left, right, target)
    block = x_blocks.shape[1]
    my_y, my_x, my_z = _blk_coords(me)
    firsts = []
    for c in range(CS):
        data = partials[c].reshape(BLK_DIMS + (block, block))
        direction = 1 if c % 2 == 0 else -1
        if c < 2:
            firsts.append(ring_reduce_scatter(data, 1, 1, direction, my_x))
        else:
            firsts.append(ring_reduce_scatter(data, 0, 0, direction, my_y))
    half = CS // 2
    along_y = direct_reduce_scatter(jnp.stack(firsts[:half]), 1, 0, my_y)
    along_x = direct_reduce_scatter(jnp.stack(firsts[half:]), 1, 1, my_x)
    results = jnp.concatenate([along_y, along_x])
    summed = pair_reduce_scatter(results, 1, my_z)
    return summed.astype(jnp.bfloat16).reshape(1, 1, CS, block, block)


def solution(mesh):
    return jax.shard_map(
        per_device,
        mesh=mesh,
        in_specs=(
            P(("blk", "grp"), None, None),
            P("blk", "grp", None, None),
            P("blk", "grp", None, None),
            P("blk", "grp", None, None),
        ),
        out_specs=P("blk", "grp", None, None, None),
        check_vma=False,
    )
```

```python
import jax
import jax.numpy as jnp
from jax import lax
from jax.experimental import pallas as pl
from jax.experimental.pallas import tpu as pltpu
from jax.sharding import PartitionSpec as P

CS = 4
OWNERS_PER_STEP = 4


def _products_kernel(left_ref, right_ref, target_ref, x_ref, *refs):
    out_refs, acc_ref = refs[:CS], refs[CS]
    step = pl.program_id(0)
    pair_count = left_ref.shape[0] // (pl.num_programs(0) * OWNERS_PER_STEP)
    acc_ref[...] = jnp.zeros_like(acc_ref)

    def body(j, carry):
        k = j // pair_count
        flat = step * OWNERS_PER_STEP * pair_count + j
        l = left_ref[flat]
        r = right_ref[flat]
        t = target_ref[flat]
        prod = lax.dot_general(
            x_ref[l], x_ref[r], (((1,), (1,)), ((), ())), preferred_element_type=jnp.float32
        )
        acc_ref[t, k] += prod
        return carry

    lax.fori_loop(0, OWNERS_PER_STEP * pair_count, body, 0, unroll=4)
    for c, out_ref in enumerate(out_refs):
        out_ref[...] = acc_ref[c]


def owner_partials(gathered, left, right, target):
    owners, pair_count = left.shape
    block = gathered.shape[1]
    steps = owners // OWNERS_PER_STEP
    flops = 2 * owners * pair_count * block * block * block
    return pl.pallas_call(
        _products_kernel,
        out_shape=[jax.ShapeDtypeStruct((owners, block, block), jnp.float32)] * CS,
        grid_spec=pltpu.PrefetchScalarGridSpec(
            num_scalar_prefetch=3,
            grid=(steps,),
            in_specs=[
                pl.BlockSpec(
                    gathered.shape,
                    lambda i, *_: (0, 0, 0),
                    pipeline_mode=pl.Buffered(1),
                )
            ],
            out_specs=[
                pl.BlockSpec((OWNERS_PER_STEP, block, block), lambda i, *_: (i, 0, 0))
            ]
            * CS,
            scratch_shapes=[pltpu.VMEM((CS, OWNERS_PER_STEP, block, block), jnp.float32)],
        ),
        compiler_params=pltpu.CompilerParams(
            dimension_semantics=("arbitrary",), vmem_limit_bytes=48 * 1024 * 1024
        ),
        cost_estimate=pl.CostEstimate(
            flops=flops,
            transcendentals=0,
            bytes_accessed=gathered.size * 2 + owners * CS * block * block * 4,
        ),
    )(left.reshape(-1), right.reshape(-1), target.reshape(-1), gathered)


BLK_DIMS = (4, 4, 2)


def _blk_coords(index):
    coords = []
    for size in reversed(BLK_DIMS):
        coords.append(index % size)
        index = index // size
    return tuple(reversed(coords))


def _blk_index(coords):
    index = 0
    for c, size in zip(coords, BLK_DIMS):
        index = index * size + c
    return index


def _shift_route(dim, step):
    route = []
    for b in range(_blk_index(tuple(s - 1 for s in BLK_DIMS)) + 1):
        coords = list(_blk_coords(b))
        coords[dim] = (coords[dim] + step) % BLK_DIMS[dim]
        route.append((b, _blk_index(tuple(coords))))
    return route


def _take(data, lead, axis, index):
    offset = len(lead)
    starts = [0] * data.ndim
    sizes = list(data.shape)
    for i, v in enumerate(lead):
        starts[i] = v
        sizes[i] = 1
    starts[offset + axis] = index
    sizes[offset + axis] = 1
    piece = lax.dynamic_slice(data, starts, sizes)
    return piece.reshape(
        [s for i, s in enumerate(sizes) if i >= offset and i != offset + axis]
    )


def ring_reduce_scatter(data, axis, dim, direction, coord, lead=()):
    size = BLK_DIMS[dim]
    route = _shift_route(dim, direction)

    def piece(k):
        return _take(data, lead, axis, (coord - direction * (1 + k)) % size)

    send = piece(0)
    for k in range(size - 1):
        arrived = lax.ppermute(send, "blk", route)
        send = arrived + piece(k + 1)
    return send


def direct_reduce_scatter(data, axis, dim, coord):
    size = BLK_DIMS[dim]
    total = lax.dynamic_index_in_dim(data, coord, axis, keepdims=False)
    for shift in range(1, size):
        piece = lax.dynamic_index_in_dim(data, (coord + shift) % size, axis, keepdims=False)
        total = total + lax.ppermute(piece, "blk", _shift_route(dim, shift))
    return total


def pair_reduce_scatter(data, axis, coord):
    route = _shift_route(2, 1)
    other = lax.dynamic_index_in_dim(data, 1 - coord, axis, keepdims=False)
    mine = lax.dynamic_index_in_dim(data, coord, axis, keepdims=False)
    return lax.ppermute(other, "blk", route) + mine


LINE, CORES = 4, 2


def line_all_gather(own):
    z = lax.axis_index("grp") // CORES
    core = lax.axis_index("grp") % CORES
    members = LINE * CORES
    up = [(g, g + CORES) for g in range(members) if g // CORES < LINE - 1]
    down = [(g, g - CORES) for g in range(members) if g // CORES > 0]
    below, above = [], []
    send_up, send_down = own, own
    for _ in range(LINE - 1):
        send_up = lax.ppermute(send_up, "grp", up)
        send_down = lax.ppermute(send_down, "grp", down)
        below.append(send_up)
        above.append(send_down)
    below = jnp.stack(below)
    above = jnp.stack(above)
    mine = []
    for spot in range(LINE):
        from_below = lax.dynamic_index_in_dim(
            below, jnp.clip(z - 1 - spot, 0, LINE - 2), 0, keepdims=False
        )
        from_above = lax.dynamic_index_in_dim(
            above, jnp.clip(spot - z - 1, 0, LINE - 2), 0, keepdims=False
        )
        mine.append(
            jnp.where(spot == z, own, jnp.where(spot < z, from_below, from_above))
        )
    mine = jnp.stack(mine)
    sibling = [(g, g ^ 1) for g in range(members)]
    theirs = lax.ppermute(mine, "grp", sibling)
    first = jnp.where(core == 0, mine, theirs)
    second = jnp.where(core == 0, theirs, mine)
    gathered = jnp.stack([first, second], axis=1)
    return gathered.reshape((members * own.shape[0],) + own.shape[1:])


def per_device(x_blocks, pair_left, pair_right, pair_target):
    assert lax.axis_size("grp") == LINE * CORES
    gathered = line_all_gather(jnp.swapaxes(x_blocks, 1, 2))
    group_count = lax.axis_size("blk")
    assert group_count == BLK_DIMS[0] * BLK_DIMS[1] * BLK_DIMS[2]
    me = lax.axis_index("blk")
    visit = (me - 1 - jnp.arange(group_count, dtype=jnp.int32)) % group_count
    left = jnp.take(pair_left[0, 0], visit, axis=0)
    right = jnp.take(pair_right[0, 0], visit, axis=0)
    target = jnp.take(pair_target[0, 0], visit, axis=0)
    partials = owner_partials(gathered, left, right, target)
    block = x_blocks.shape[1]
    my_y, my_x, my_z = _blk_coords(me)
    firsts = []
    for c in range(CS):
        data = partials[c].reshape(BLK_DIMS + (block, block))
        direction = 1 if c % 2 == 0 else -1
        if c < 2:
            firsts.append(ring_reduce_scatter(data, 1, 1, direction, my_x))
        else:
            firsts.append(ring_reduce_scatter(data, 0, 0, direction, my_y))
    half = CS // 2
    along_y = direct_reduce_scatter(jnp.stack(firsts[:half]), 1, 0, my_y)
    along_x = direct_reduce_scatter(jnp.stack(firsts[half:]), 1, 1, my_x)
    results = jnp.concatenate([along_y, along_x])
    summed = pair_reduce_scatter(results, 1, my_z)
    return summed.astype(jnp.bfloat16).reshape(1, 1, CS, block, block)


def solution(mesh):
    return jax.shard_map(
        per_device,
        mesh=mesh,
        in_specs=(
            P(("blk", "grp"), None, None),
            P("blk", "grp", None, None),
            P("blk", "grp", None, None),
            P("blk", "grp", None, None),
        ),
        out_specs=P("blk", "grp", None, None, None),
        check_vma=False,
    )
```

```python
import jax
import jax.numpy as jnp
from jax import lax
from jax.experimental import pallas as pl
from jax.experimental.pallas import tpu as pltpu
from jax.sharding import PartitionSpec as P

CS = 4
OWNERS_PER_STEP = 4


def _products_kernel(left_ref, right_ref, target_ref, x_ref, *refs):
    out_refs, acc_ref = refs[:CS], refs[CS]
    step = pl.program_id(0)
    pair_count = left_ref.shape[0] // (pl.num_programs(0) * OWNERS_PER_STEP)
    acc_ref[...] = jnp.zeros_like(acc_ref)

    def body(j, carry):
        k = j // pair_count
        flat = step * OWNERS_PER_STEP * pair_count + j
        l = left_ref[flat]
        r = right_ref[flat]
        t = target_ref[flat]
        prod = lax.dot_general(
            x_ref[l], x_ref[r], (((0,), (0,)), ((), ())), preferred_element_type=jnp.float32
        )
        acc_ref[t, k] += prod
        return carry

    lax.fori_loop(0, OWNERS_PER_STEP * pair_count, body, 0, unroll=4)
    for c, out_ref in enumerate(out_refs):
        out_ref[...] = acc_ref[c]


def owner_partials(gathered, left, right, target):
    owners, pair_count = left.shape
    block = gathered.shape[1]
    steps = owners // OWNERS_PER_STEP
    flops = 2 * owners * pair_count * block * block * block
    return pl.pallas_call(
        _products_kernel,
        out_shape=[jax.ShapeDtypeStruct((owners, block, block), jnp.float32)] * CS,
        grid_spec=pltpu.PrefetchScalarGridSpec(
            num_scalar_prefetch=3,
            grid=(steps,),
            in_specs=[
                pl.BlockSpec(
                    gathered.shape,
                    lambda i, *_: (0, 0, 0),
                    pipeline_mode=pl.Buffered(1),
                )
            ],
            out_specs=[
                pl.BlockSpec((OWNERS_PER_STEP, block, block), lambda i, *_: (i, 0, 0))
            ]
            * CS,
            scratch_shapes=[pltpu.VMEM((CS, OWNERS_PER_STEP, block, block), jnp.float32)],
        ),
        compiler_params=pltpu.CompilerParams(
            dimension_semantics=("arbitrary",), vmem_limit_bytes=48 * 1024 * 1024
        ),
        cost_estimate=pl.CostEstimate(
            flops=flops,
            transcendentals=0,
            bytes_accessed=gathered.size * 2 + owners * CS * block * block * 4,
        ),
    )(left.reshape(-1), right.reshape(-1), target.reshape(-1), gathered)


BLK_DIMS = (4, 4, 2)


def _blk_coords(index):
    coords = []
    for size in reversed(BLK_DIMS):
        coords.append(index % size)
        index = index // size
    return tuple(reversed(coords))


def _blk_index(coords):
    index = 0
    for c, size in zip(coords, BLK_DIMS):
        index = index * size + c
    return index


def _shift_route(dim, step):
    route = []
    for b in range(_blk_index(tuple(s - 1 for s in BLK_DIMS)) + 1):
        coords = list(_blk_coords(b))
        coords[dim] = (coords[dim] + step) % BLK_DIMS[dim]
        route.append((b, _blk_index(tuple(coords))))
    return route


def _take(data, lead, axis, index):
    offset = len(lead)
    starts = [0] * data.ndim
    sizes = list(data.shape)
    for i, v in enumerate(lead):
        starts[i] = v
        sizes[i] = 1
    starts[offset + axis] = index
    sizes[offset + axis] = 1
    piece = lax.dynamic_slice(data, starts, sizes)
    return piece.reshape(
        [s for i, s in enumerate(sizes) if i >= offset and i != offset + axis]
    )


def ring_reduce_scatter(data, axis, dim, direction, coord, lead=()):
    size = BLK_DIMS[dim]
    route = _shift_route(dim, direction)

    def piece(k):
        return _take(data, lead, axis, (coord - direction * (1 + k)) % size)

    send = piece(0)
    for k in range(size - 1):
        arrived = lax.ppermute(send, "blk", route)
        send = arrived + piece(k + 1)
    return send


def direct_reduce_scatter(data, axis, dim, coord):
    size = BLK_DIMS[dim]
    total = lax.dynamic_index_in_dim(data, coord, axis, keepdims=False)
    for shift in range(1, size):
        piece = lax.dynamic_index_in_dim(data, (coord + shift) % size, axis, keepdims=False)
        total = total + lax.ppermute(piece, "blk", _shift_route(dim, shift))
    return total


def pair_reduce_scatter(data, axis, coord):
    route = _shift_route(2, 1)
    other = lax.dynamic_index_in_dim(data, 1 - coord, axis, keepdims=False)
    mine = lax.dynamic_index_in_dim(data, coord, axis, keepdims=False)
    return lax.ppermute(other, "blk", route) + mine


LINE, CORES = 4, 2


def line_all_gather(own):
    z = lax.axis_index("grp") // CORES
    core = lax.axis_index("grp") % CORES
    members = LINE * CORES
    sibling = [(g, g ^ 1) for g in range(members)]
    other = lax.ppermute(own, "grp", sibling)
    chip = jnp.stack([jnp.where(core == 0, own, other), jnp.where(core == 0, other, own)])
    route = [(g, g + CORES) for g in range(0, members - CORES, CORES)]
    route += [(g, g - CORES) for g in range(CORES + 1, members, CORES)]
    carried = []
    send = chip
    for _ in range(LINE - 1):
        send = lax.ppermute(send, "grp", route)
        carried.append(send)
    carried = jnp.stack(carried)
    swapped = lax.ppermute(carried, "grp", sibling)
    below = jnp.where(core == 0, carried, swapped)
    above = jnp.where(core == 0, swapped, carried)
    rows = []
    for spot in range(LINE):
        from_below = lax.dynamic_index_in_dim(
            below, jnp.clip(z - 1 - spot, 0, LINE - 2), 0, keepdims=False
        )
        from_above = lax.dynamic_index_in_dim(
            above, jnp.clip(spot - z - 1, 0, LINE - 2), 0, keepdims=False
        )
        rows.append(jnp.where(spot == z, chip, jnp.where(spot < z, from_below, from_above)))
    gathered = jnp.stack(rows)
    return gathered.reshape((members * own.shape[0],) + own.shape[1:])


def per_device(x_blocks, pair_left, pair_right, pair_target):
    assert lax.axis_size("grp") == LINE * CORES
    gathered = line_all_gather(x_blocks)
    group_count = lax.axis_size("blk")
    assert group_count == BLK_DIMS[0] * BLK_DIMS[1] * BLK_DIMS[2]
    me = lax.axis_index("blk")
    visit = (me - 1 - jnp.arange(group_count, dtype=jnp.int32)) % group_count
    left = jnp.take(pair_left[0, 0], visit, axis=0)
    right = jnp.take(pair_right[0, 0], visit, axis=0)
    target = jnp.take(pair_target[0, 0], visit, axis=0)
    partials = owner_partials(gathered, left, right, target)
    block = x_blocks.shape[1]
    my_y, my_x, my_z = _blk_coords(me)
    firsts = []
    for c in range(CS):
        data = partials[c].reshape(BLK_DIMS + (block, block))
        direction = 1 if c % 2 == 0 else -1
        if c < 2:
            firsts.append(ring_reduce_scatter(data, 1, 1, direction, my_x))
        else:
            firsts.append(ring_reduce_scatter(data, 0, 0, direction, my_y))
    half = CS // 2
    along_y = direct_reduce_scatter(jnp.stack(firsts[:half]), 1, 0, my_y)
    along_x = direct_reduce_scatter(jnp.stack(firsts[half:]), 1, 1, my_x)
    results = jnp.concatenate([along_y, along_x])
    summed = pair_reduce_scatter(results, 1, my_z)
    return summed.astype(jnp.bfloat16).reshape(1, 1, CS, block, block)


def solution(mesh):
    return jax.shard_map(
        per_device,
        mesh=mesh,
        in_specs=(
            P(("blk", "grp"), None, None),
            P("blk", "grp", None, None),
            P("blk", "grp", None, None),
            P("blk", "grp", None, None),
        ),
        out_specs=P("blk", "grp", None, None, None),
        check_vma=False,
    )
```

```python
import jax
import jax.numpy as jnp
from jax import lax
from jax.experimental import pallas as pl
from jax.experimental.pallas import tpu as pltpu
from jax.sharding import PartitionSpec as P

CS = 4
OWNERS_PER_STEP = 4


def _products_kernel(left_ref, right_ref, target_ref, x_ref, *refs):
    out_refs, acc_ref = refs[:CS], refs[CS]
    step = pl.program_id(0)
    pair_count = left_ref.shape[0] // (pl.num_programs(0) * OWNERS_PER_STEP)
    acc_ref[...] = jnp.zeros_like(acc_ref)

    def body(j, carry):
        k = j // pair_count
        flat = step * OWNERS_PER_STEP * pair_count + j
        l = left_ref[flat]
        r = right_ref[flat]
        t = target_ref[flat]
        prod = lax.dot_general(
            x_ref[l], x_ref[r], (((0,), (0,)), ((), ())), preferred_element_type=jnp.float32
        )
        acc_ref[t, k] += prod
        return carry

    lax.fori_loop(0, OWNERS_PER_STEP * pair_count, body, 0, unroll=4)
    for c, out_ref in enumerate(out_refs):
        out_ref[...] = acc_ref[c]


def owner_partials(gathered, left, right, target):
    owners, pair_count = left.shape
    block = gathered.shape[1]
    steps = owners // OWNERS_PER_STEP
    flops = 2 * owners * pair_count * block * block * block
    return pl.pallas_call(
        _products_kernel,
        out_shape=[jax.ShapeDtypeStruct((owners, block, block), jnp.float32)] * CS,
        grid_spec=pltpu.PrefetchScalarGridSpec(
            num_scalar_prefetch=3,
            grid=(steps,),
            in_specs=[
                pl.BlockSpec(
                    gathered.shape,
                    lambda i, *_: (0, 0, 0),
                    pipeline_mode=pl.Buffered(1),
                )
            ],
            out_specs=[
                pl.BlockSpec((OWNERS_PER_STEP, block, block), lambda i, *_: (i, 0, 0))
            ]
            * CS,
            scratch_shapes=[pltpu.VMEM((CS, OWNERS_PER_STEP, block, block), jnp.float32)],
        ),
        compiler_params=pltpu.CompilerParams(
            dimension_semantics=("arbitrary",), vmem_limit_bytes=48 * 1024 * 1024
        ),
        cost_estimate=pl.CostEstimate(
            flops=flops,
            transcendentals=0,
            bytes_accessed=gathered.size * 2 + owners * CS * block * block * 4,
        ),
    )(left.reshape(-1), right.reshape(-1), target.reshape(-1), gathered)


BLK_DIMS = (4, 4, 2)


def _blk_coords(index):
    coords = []
    for size in reversed(BLK_DIMS):
        coords.append(index % size)
        index = index // size
    return tuple(reversed(coords))


def _blk_index(coords):
    index = 0
    for c, size in zip(coords, BLK_DIMS):
        index = index * size + c
    return index


def _shift_route(dim, step):
    route = []
    for b in range(_blk_index(tuple(s - 1 for s in BLK_DIMS)) + 1):
        coords = list(_blk_coords(b))
        coords[dim] = (coords[dim] + step) % BLK_DIMS[dim]
        route.append((b, _blk_index(tuple(coords))))
    return route


def _take(data, lead, axis, index):
    offset = len(lead)
    starts = [0] * data.ndim
    sizes = list(data.shape)
    for i, v in enumerate(lead):
        starts[i] = v
        sizes[i] = 1
    starts[offset + axis] = index
    sizes[offset + axis] = 1
    piece = lax.dynamic_slice(data, starts, sizes)
    return piece.reshape(
        [s for i, s in enumerate(sizes) if i >= offset and i != offset + axis]
    )


def ring_reduce_scatter(data, axis, dim, direction, coord, lead=()):
    size = BLK_DIMS[dim]
    route = _shift_route(dim, direction)

    def piece(k):
        return _take(data, lead, axis, (coord - direction * (1 + k)) % size)

    send = piece(0)
    for k in range(size - 1):
        arrived = lax.ppermute(send, "blk", route)
        send = arrived + piece(k + 1)
    return send


def direct_reduce_scatter(data, axis, dim, coord):
    size = BLK_DIMS[dim]
    total = lax.dynamic_index_in_dim(data, coord, axis, keepdims=False)
    for shift in range(1, size):
        piece = lax.dynamic_index_in_dim(data, (coord + shift) % size, axis, keepdims=False)
        total = total + lax.ppermute(piece, "blk", _shift_route(dim, shift))
    return total


def pair_reduce_scatter(data, axis, coord):
    route = _shift_route(2, 1)
    other = lax.dynamic_index_in_dim(data, 1 - coord, axis, keepdims=False)
    mine = lax.dynamic_index_in_dim(data, coord, axis, keepdims=False)
    return lax.ppermute(other, "blk", route) + mine


LINE, CORES = 4, 2


def line_all_gather(own):
    z = lax.axis_index("grp") // CORES
    core = lax.axis_index("grp") % CORES
    members = LINE * CORES
    up = [(g, g + CORES) for g in range(members) if g // CORES < LINE - 1]
    down = [(g, g - CORES) for g in range(members) if g // CORES > 0]
    below, above = [], []
    send_up, send_down = own, own
    for _ in range(LINE - 1):
        send_up = lax.ppermute(send_up, "grp", up)
        send_down = lax.ppermute(send_down, "grp", down)
        below.append(send_up)
        above.append(send_down)
    below = jnp.stack(below)
    above = jnp.stack(above)
    mine = []
    for spot in range(LINE):
        from_below = lax.dynamic_index_in_dim(
            below, jnp.clip(z - 1 - spot, 0, LINE - 2), 0, keepdims=False
        )
        from_above = lax.dynamic_index_in_dim(
            above, jnp.clip(spot - z - 1, 0, LINE - 2), 0, keepdims=False
        )
        mine.append(
            jnp.where(spot == z, own, jnp.where(spot < z, from_below, from_above))
        )
    mine = jnp.stack(mine)
    sibling = [(g, g ^ 1) for g in range(members)]
    theirs = lax.ppermute(mine, "grp", sibling)
    first = jnp.where(core == 0, mine, theirs)
    second = jnp.where(core == 0, theirs, mine)
    gathered = jnp.stack([first, second], axis=1)
    return gathered.reshape((members * own.shape[0],) + own.shape[1:])


def per_device(x_blocks, pair_left, pair_right, pair_target):
    assert lax.axis_size("grp") == LINE * CORES
    gathered = line_all_gather(x_blocks)
    group_count = lax.axis_size("blk")
    assert group_count == BLK_DIMS[0] * BLK_DIMS[1] * BLK_DIMS[2]
    me = lax.axis_index("blk")
    visit = (me - 1 - jnp.arange(group_count, dtype=jnp.int32)) % group_count
    left = jnp.take(pair_left[0, 0], visit, axis=0)
    right = jnp.take(pair_right[0, 0], visit, axis=0)
    target = jnp.take(pair_target[0, 0], visit, axis=0)
    partials = owner_partials(gathered, left, right, target)
    block = x_blocks.shape[1]
    my_y, my_x, my_z = _blk_coords(me)
    firsts = []
    rows = block // 2
    for c in range(CS):
        data = partials[c].reshape(BLK_DIMS + (block, block))
        direction = 1 if c % 2 == 0 else -1
        halves = []
        for h in range(2):
            part = data[..., h * rows : (h + 1) * rows, :]
            if c < 2:
                halves.append(ring_reduce_scatter(part, 1, 1, direction, my_x))
            else:
                halves.append(ring_reduce_scatter(part, 0, 0, direction, my_y))
        firsts.append(jnp.concatenate(halves, axis=-2))
    half = CS // 2
    along_y = direct_reduce_scatter(jnp.stack(firsts[:half]), 1, 0, my_y)
    along_x = direct_reduce_scatter(jnp.stack(firsts[half:]), 1, 1, my_x)
    results = jnp.concatenate([along_y, along_x])
    summed = pair_reduce_scatter(results, 1, my_z)
    return summed.astype(jnp.bfloat16).reshape(1, 1, CS, block, block)


def solution(mesh):
    return jax.shard_map(
        per_device,
        mesh=mesh,
        in_specs=(
            P(("blk", "grp"), None, None),
            P("blk", "grp", None, None),
            P("blk", "grp", None, None),
            P("blk", "grp", None, None),
        ),
        out_specs=P("blk", "grp", None, None, None),
        check_vma=False,
    )
```

```python
import jax
import jax.numpy as jnp
from jax import lax
from jax.experimental import pallas as pl
from jax.experimental.pallas import tpu as pltpu
from jax.sharding import PartitionSpec as P

CS = 4
OWNERS_PER_STEP = 4
ROW_PARTS = 2


def _products_kernel(left_ref, right_ref, target_ref, x_ref, *refs):
    out_refs, acc_ref = refs[: CS * ROW_PARTS], refs[CS * ROW_PARTS]
    step = pl.program_id(0)
    pair_count = left_ref.shape[0] // (pl.num_programs(0) * OWNERS_PER_STEP)
    acc_ref[...] = jnp.zeros_like(acc_ref)

    def body(j, carry):
        k = j // pair_count
        flat = step * OWNERS_PER_STEP * pair_count + j
        l = left_ref[flat]
        r = right_ref[flat]
        t = target_ref[flat]
        prod = lax.dot_general(
            x_ref[l], x_ref[r], (((0,), (0,)), ((), ())), preferred_element_type=jnp.float32
        )
        acc_ref[t, k] += prod
        return carry

    lax.fori_loop(0, OWNERS_PER_STEP * pair_count, body, 0, unroll=4)
    rows = acc_ref.shape[2] // ROW_PARTS
    for n, out_ref in enumerate(out_refs):
        c, h = divmod(n, ROW_PARTS)
        out_ref[...] = acc_ref[c, :, h * rows : (h + 1) * rows, :]


def owner_partials(gathered, left, right, target):
    owners, pair_count = left.shape
    block = gathered.shape[1]
    steps = owners // OWNERS_PER_STEP
    flops = 2 * owners * pair_count * block * block * block
    return pl.pallas_call(
        _products_kernel,
        out_shape=[jax.ShapeDtypeStruct((owners, block // ROW_PARTS, block), jnp.float32)]
        * (CS * ROW_PARTS),
        grid_spec=pltpu.PrefetchScalarGridSpec(
            num_scalar_prefetch=3,
            grid=(steps,),
            in_specs=[
                pl.BlockSpec(
                    gathered.shape,
                    lambda i, *_: (0, 0, 0),
                    pipeline_mode=pl.Buffered(1),
                )
            ],
            out_specs=[
                pl.BlockSpec(
                    (OWNERS_PER_STEP, block // ROW_PARTS, block), lambda i, *_: (i, 0, 0)
                )
            ]
            * (CS * ROW_PARTS),
            scratch_shapes=[pltpu.VMEM((CS, OWNERS_PER_STEP, block, block), jnp.float32)],
        ),
        compiler_params=pltpu.CompilerParams(
            dimension_semantics=("arbitrary",), vmem_limit_bytes=48 * 1024 * 1024
        ),
        cost_estimate=pl.CostEstimate(
            flops=flops,
            transcendentals=0,
            bytes_accessed=gathered.size * 2 + owners * CS * block * block * 4,
        ),
    )(left.reshape(-1), right.reshape(-1), target.reshape(-1), gathered)


BLK_DIMS = (4, 4, 2)


def _blk_coords(index):
    coords = []
    for size in reversed(BLK_DIMS):
        coords.append(index % size)
        index = index // size
    return tuple(reversed(coords))


def _blk_index(coords):
    index = 0
    for c, size in zip(coords, BLK_DIMS):
        index = index * size + c
    return index


def _shift_route(dim, step):
    route = []
    for b in range(_blk_index(tuple(s - 1 for s in BLK_DIMS)) + 1):
        coords = list(_blk_coords(b))
        coords[dim] = (coords[dim] + step) % BLK_DIMS[dim]
        route.append((b, _blk_index(tuple(coords))))
    return route


def _take(data, lead, axis, index):
    offset = len(lead)
    starts = [0] * data.ndim
    sizes = list(data.shape)
    for i, v in enumerate(lead):
        starts[i] = v
        sizes[i] = 1
    starts[offset + axis] = index
    sizes[offset + axis] = 1
    piece = lax.dynamic_slice(data, starts, sizes)
    return piece.reshape(
        [s for i, s in enumerate(sizes) if i >= offset and i != offset + axis]
    )


def ring_reduce_scatter(data, axis, dim, direction, coord, lead=()):
    size = BLK_DIMS[dim]
    route = _shift_route(dim, direction)

    def piece(k):
        return _take(data, lead, axis, (coord - direction * (1 + k)) % size)

    send = piece(0)
    for k in range(size - 1):
        arrived = lax.ppermute(send, "blk", route)
        send = arrived + piece(k + 1)
    return send


def direct_reduce_scatter(data, axis, dim, coord):
    size = BLK_DIMS[dim]
    total = lax.dynamic_index_in_dim(data, coord, axis, keepdims=False)
    for shift in range(1, size):
        piece = lax.dynamic_index_in_dim(data, (coord + shift) % size, axis, keepdims=False)
        total = total + lax.ppermute(piece, "blk", _shift_route(dim, shift))
    return total


def pair_reduce_scatter(data, axis, coord):
    route = _shift_route(2, 1)
    other = lax.dynamic_index_in_dim(data, 1 - coord, axis, keepdims=False)
    mine = lax.dynamic_index_in_dim(data, coord, axis, keepdims=False)
    return lax.ppermute(other, "blk", route) + mine


LINE, CORES = 4, 2


def line_all_gather(own):
    z = lax.axis_index("grp") // CORES
    core = lax.axis_index("grp") % CORES
    members = LINE * CORES
    up = [(g, g + CORES) for g in range(members) if g // CORES < LINE - 1]
    down = [(g, g - CORES) for g in range(members) if g // CORES > 0]
    below, above = [], []
    send_up, send_down = own, own
    for _ in range(LINE - 1):
        send_up = lax.ppermute(send_up, "grp", up)
        send_down = lax.ppermute(send_down, "grp", down)
        below.append(send_up)
        above.append(send_down)
    below = jnp.stack(below)
    above = jnp.stack(above)
    mine = []
    for spot in range(LINE):
        from_below = lax.dynamic_index_in_dim(
            below, jnp.clip(z - 1 - spot, 0, LINE - 2), 0, keepdims=False
        )
        from_above = lax.dynamic_index_in_dim(
            above, jnp.clip(spot - z - 1, 0, LINE - 2), 0, keepdims=False
        )
        mine.append(
            jnp.where(spot == z, own, jnp.where(spot < z, from_below, from_above))
        )
    mine = jnp.stack(mine)
    sibling = [(g, g ^ 1) for g in range(members)]
    theirs = lax.ppermute(mine, "grp", sibling)
    first = jnp.where(core == 0, mine, theirs)
    second = jnp.where(core == 0, theirs, mine)
    gathered = jnp.stack([first, second], axis=1)
    return gathered.reshape((members * own.shape[0],) + own.shape[1:])


def per_device(x_blocks, pair_left, pair_right, pair_target):
    assert lax.axis_size("grp") == LINE * CORES
    gathered = line_all_gather(x_blocks)
    group_count = lax.axis_size("blk")
    assert group_count == BLK_DIMS[0] * BLK_DIMS[1] * BLK_DIMS[2]
    me = lax.axis_index("blk")
    visit = (me - 1 - jnp.arange(group_count, dtype=jnp.int32)) % group_count
    left = jnp.take(pair_left[0, 0], visit, axis=0)
    right = jnp.take(pair_right[0, 0], visit, axis=0)
    target = jnp.take(pair_target[0, 0], visit, axis=0)
    partials = owner_partials(gathered, left, right, target)
    block = x_blocks.shape[1]
    my_y, my_x, my_z = _blk_coords(me)
    firsts = []
    rows = block // ROW_PARTS
    for c in range(CS):
        direction = 1 if c % 2 == 0 else -1
        halves = []
        for h in range(ROW_PARTS):
            part = partials[c * ROW_PARTS + h].reshape(BLK_DIMS + (rows, block))
            if c < 2:
                halves.append(ring_reduce_scatter(part, 1, 1, direction, my_x))
            else:
                halves.append(ring_reduce_scatter(part, 0, 0, direction, my_y))
        firsts.append(jnp.concatenate(halves, axis=-2))
    half = CS // 2
    along_y = direct_reduce_scatter(jnp.stack(firsts[:half]), 1, 0, my_y)
    along_x = direct_reduce_scatter(jnp.stack(firsts[half:]), 1, 1, my_x)
    results = jnp.concatenate([along_y, along_x])
    summed = pair_reduce_scatter(results, 1, my_z)
    return summed.astype(jnp.bfloat16).reshape(1, 1, CS, block, block)


def solution(mesh):
    return jax.shard_map(
        per_device,
        mesh=mesh,
        in_specs=(
            P(("blk", "grp"), None, None),
            P("blk", "grp", None, None),
            P("blk", "grp", None, None),
            P("blk", "grp", None, None),
        ),
        out_specs=P("blk", "grp", None, None, None),
        check_vma=False,
    )
```

```python
import jax
import jax.numpy as jnp
from jax import lax
from jax.experimental import pallas as pl
from jax.experimental.pallas import tpu as pltpu
from jax.sharding import PartitionSpec as P

CS = 4
OWNERS_PER_STEP = 4
ROW_PARTS = 2


def _products_kernel(left_ref, right_ref, target_ref, x_ref, *refs):
    out_refs, acc_ref = refs[: CS * ROW_PARTS], refs[CS * ROW_PARTS]
    step = pl.program_id(0)
    pair_count = left_ref.shape[0] // (pl.num_programs(0) * OWNERS_PER_STEP)
    acc_ref[...] = jnp.zeros_like(acc_ref)

    def body(j, carry):
        k = j // pair_count
        flat = step * OWNERS_PER_STEP * pair_count + j
        l = left_ref[flat]
        r = right_ref[flat]
        t = target_ref[flat]
        prod = lax.dot_general(
            x_ref[l], x_ref[r], (((0,), (0,)), ((), ())), preferred_element_type=jnp.float32
        )
        acc_ref[t, k] += prod
        return carry

    lax.fori_loop(0, OWNERS_PER_STEP * pair_count, body, 0, unroll=4)
    rows = acc_ref.shape[2] // ROW_PARTS
    for n, out_ref in enumerate(out_refs):
        c, h = divmod(n, ROW_PARTS)
        out_ref[...] = acc_ref[c, :, h * rows : (h + 1) * rows, :]


def owner_partials(gathered, left, right, target):
    owners, pair_count = left.shape
    block = gathered.shape[1]
    steps = owners // OWNERS_PER_STEP
    flops = 2 * owners * pair_count * block * block * block
    return pl.pallas_call(
        _products_kernel,
        out_shape=[jax.ShapeDtypeStruct((owners, block // ROW_PARTS, block), jnp.float32)]
        * (CS * ROW_PARTS),
        grid_spec=pltpu.PrefetchScalarGridSpec(
            num_scalar_prefetch=3,
            grid=(steps,),
            in_specs=[
                pl.BlockSpec(
                    gathered.shape,
                    lambda i, *_: (0, 0, 0),
                    pipeline_mode=pl.Buffered(1),
                )
            ],
            out_specs=[
                pl.BlockSpec(
                    (OWNERS_PER_STEP, block // ROW_PARTS, block), lambda i, *_: (i, 0, 0)
                )
            ]
            * (CS * ROW_PARTS),
            scratch_shapes=[pltpu.VMEM((CS, OWNERS_PER_STEP, block, block), jnp.float32)],
        ),
        compiler_params=pltpu.CompilerParams(
            dimension_semantics=("arbitrary",), vmem_limit_bytes=48 * 1024 * 1024
        ),
        cost_estimate=pl.CostEstimate(
            flops=flops,
            transcendentals=0,
            bytes_accessed=gathered.size * 2 + owners * CS * block * block * 4,
        ),
    )(left.reshape(-1), right.reshape(-1), target.reshape(-1), gathered)


BLK_DIMS = (4, 4, 2)


def _blk_coords(index):
    coords = []
    for size in reversed(BLK_DIMS):
        coords.append(index % size)
        index = index // size
    return tuple(reversed(coords))


def _blk_index(coords):
    index = 0
    for c, size in zip(coords, BLK_DIMS):
        index = index * size + c
    return index


def _shift_route(dim, step):
    route = []
    for b in range(_blk_index(tuple(s - 1 for s in BLK_DIMS)) + 1):
        coords = list(_blk_coords(b))
        coords[dim] = (coords[dim] + step) % BLK_DIMS[dim]
        route.append((b, _blk_index(tuple(coords))))
    return route


def _take(data, lead, axis, index):
    offset = len(lead)
    starts = [0] * data.ndim
    sizes = list(data.shape)
    for i, v in enumerate(lead):
        starts[i] = v
        sizes[i] = 1
    starts[offset + axis] = index
    sizes[offset + axis] = 1
    piece = lax.dynamic_slice(data, starts, sizes)
    return piece.reshape(
        [s for i, s in enumerate(sizes) if i >= offset and i != offset + axis]
    )


def ring_reduce_scatter(data, axis, dim, direction, coord, lead=()):
    size = BLK_DIMS[dim]
    route = _shift_route(dim, direction)

    def piece(k):
        return _take(data, lead, axis, (coord - direction * (1 + k)) % size)

    send = piece(0)
    for k in range(size - 1):
        arrived = lax.ppermute(send, "blk", route)
        send = arrived + piece(k + 1)
    return send


def direct_reduce_scatter(data, axis, dim, coord):
    size = BLK_DIMS[dim]
    total = lax.dynamic_index_in_dim(data, coord, axis, keepdims=False)
    for shift in range(1, size):
        piece = lax.dynamic_index_in_dim(data, (coord + shift) % size, axis, keepdims=False)
        total = total + lax.ppermute(piece, "blk", _shift_route(dim, shift))
    return total


def pair_reduce_scatter(data, axis, coord):
    route = _shift_route(2, 1)
    other = lax.dynamic_index_in_dim(data, 1 - coord, axis, keepdims=False)
    mine = lax.dynamic_index_in_dim(data, coord, axis, keepdims=False)
    return lax.ppermute(other, "blk", route) + mine


LINE, CORES = 4, 2


def line_all_gather(own):
    z = lax.axis_index("grp") // CORES
    core = lax.axis_index("grp") % CORES
    members = LINE * CORES
    up = [(g, g + CORES) for g in range(members) if g // CORES < LINE - 1]
    down = [(g, g - CORES) for g in range(members) if g // CORES > 0]
    half = own.shape[0] // 2
    chains = []
    for part in (own[:half], own[half:]):
        got_below, got_above = [], []
        send_up, send_down = part, part
        for _ in range(LINE - 1):
            send_up = lax.ppermute(send_up, "grp", up)
            send_down = lax.ppermute(send_down, "grp", down)
            got_below.append(send_up)
            got_above.append(send_down)
        chains.append((jnp.stack(got_below), jnp.stack(got_above)))
    below = jnp.concatenate([chains[0][0], chains[1][0]], axis=1)
    above = jnp.concatenate([chains[0][1], chains[1][1]], axis=1)
    mine = []
    for spot in range(LINE):
        from_below = lax.dynamic_index_in_dim(
            below, jnp.clip(z - 1 - spot, 0, LINE - 2), 0, keepdims=False
        )
        from_above = lax.dynamic_index_in_dim(
            above, jnp.clip(spot - z - 1, 0, LINE - 2), 0, keepdims=False
        )
        mine.append(
            jnp.where(spot == z, own, jnp.where(spot < z, from_below, from_above))
        )
    mine = jnp.stack(mine)
    sibling = [(g, g ^ 1) for g in range(members)]
    theirs = lax.ppermute(mine, "grp", sibling)
    first = jnp.where(core == 0, mine, theirs)
    second = jnp.where(core == 0, theirs, mine)
    gathered = jnp.stack([first, second], axis=1)
    return gathered.reshape((members * own.shape[0],) + own.shape[1:])


def per_device(x_blocks, pair_left, pair_right, pair_target):
    assert lax.axis_size("grp") == LINE * CORES
    gathered = line_all_gather(x_blocks)
    group_count = lax.axis_size("blk")
    assert group_count == BLK_DIMS[0] * BLK_DIMS[1] * BLK_DIMS[2]
    me = lax.axis_index("blk")
    visit = (me - 1 - jnp.arange(group_count, dtype=jnp.int32)) % group_count
    left = jnp.take(pair_left[0, 0], visit, axis=0)
    right = jnp.take(pair_right[0, 0], visit, axis=0)
    target = jnp.take(pair_target[0, 0], visit, axis=0)
    partials = owner_partials(gathered, left, right, target)
    block = x_blocks.shape[1]
    my_y, my_x, my_z = _blk_coords(me)
    firsts = []
    rows = block // ROW_PARTS
    for c in range(CS):
        direction = 1 if c % 2 == 0 else -1
        halves = []
        for h in range(ROW_PARTS):
            part = partials[c * ROW_PARTS + h].reshape(BLK_DIMS + (rows, block))
            if c < 2:
                halves.append(ring_reduce_scatter(part, 1, 1, direction, my_x))
            else:
                halves.append(ring_reduce_scatter(part, 0, 0, direction, my_y))
        firsts.append(jnp.concatenate(halves, axis=-2))
    half = CS // 2
    along_y = direct_reduce_scatter(jnp.stack(firsts[:half]), 1, 0, my_y)
    along_x = direct_reduce_scatter(jnp.stack(firsts[half:]), 1, 1, my_x)
    results = jnp.concatenate([along_y, along_x])
    summed = pair_reduce_scatter(results, 1, my_z)
    return summed.astype(jnp.bfloat16).reshape(1, 1, CS, block, block)


def solution(mesh):
    return jax.shard_map(
        per_device,
        mesh=mesh,
        in_specs=(
            P(("blk", "grp"), None, None),
            P("blk", "grp", None, None),
            P("blk", "grp", None, None),
            P("blk", "grp", None, None),
        ),
        out_specs=P("blk", "grp", None, None, None),
        check_vma=False,
    )
```

```python
import jax
import jax.numpy as jnp
from jax import lax
from jax.experimental import pallas as pl
from jax.experimental.pallas import tpu as pltpu
from jax.sharding import PartitionSpec as P

CS = 4
OWNERS_PER_STEP = 4
ROW_PARTS = 2


def _products_kernel(left_ref, right_ref, target_ref, x_ref, *refs):
    out_refs, acc_ref = refs[: CS * ROW_PARTS], refs[CS * ROW_PARTS]
    step = pl.program_id(0)
    pair_count = left_ref.shape[0] // (pl.num_programs(0) * OWNERS_PER_STEP)
    acc_ref[...] = jnp.zeros_like(acc_ref)

    def body(j, carry):
        k = j // pair_count
        flat = step * OWNERS_PER_STEP * pair_count + j
        l = left_ref[flat]
        r = right_ref[flat]
        t = target_ref[flat]
        prod = lax.dot_general(
            x_ref[l], x_ref[r], (((0,), (0,)), ((), ())), preferred_element_type=jnp.float32
        )
        acc_ref[t, k] += prod
        return carry

    lax.fori_loop(0, OWNERS_PER_STEP * pair_count, body, 0, unroll=4)
    rows = acc_ref.shape[2] // ROW_PARTS
    for n, out_ref in enumerate(out_refs):
        c, h = divmod(n, ROW_PARTS)
        out_ref[...] = acc_ref[c, :, h * rows : (h + 1) * rows, :]


def owner_partials(gathered, left, right, target):
    owners, pair_count = left.shape
    block = gathered.shape[1]
    steps = owners // OWNERS_PER_STEP
    flops = 2 * owners * pair_count * block * block * block
    return pl.pallas_call(
        _products_kernel,
        out_shape=[jax.ShapeDtypeStruct((owners, block // ROW_PARTS, block), jnp.float32)]
        * (CS * ROW_PARTS),
        grid_spec=pltpu.PrefetchScalarGridSpec(
            num_scalar_prefetch=3,
            grid=(steps,),
            in_specs=[
                pl.BlockSpec(
                    gathered.shape,
                    lambda i, *_: (0, 0, 0),
                    pipeline_mode=pl.Buffered(1),
                )
            ],
            out_specs=[
                pl.BlockSpec(
                    (OWNERS_PER_STEP, block // ROW_PARTS, block), lambda i, *_: (i, 0, 0)
                )
            ]
            * (CS * ROW_PARTS),
            scratch_shapes=[pltpu.VMEM((CS, OWNERS_PER_STEP, block, block), jnp.float32)],
        ),
        compiler_params=pltpu.CompilerParams(
            dimension_semantics=("arbitrary",), vmem_limit_bytes=48 * 1024 * 1024
        ),
        cost_estimate=pl.CostEstimate(
            flops=flops,
            transcendentals=0,
            bytes_accessed=gathered.size * 2 + owners * CS * block * block * 4,
        ),
    )(left.reshape(-1), right.reshape(-1), target.reshape(-1), gathered)


BLK_DIMS = (4, 4, 2)


def _blk_coords(index):
    coords = []
    for size in reversed(BLK_DIMS):
        coords.append(index % size)
        index = index // size
    return tuple(reversed(coords))


def _blk_index(coords):
    index = 0
    for c, size in zip(coords, BLK_DIMS):
        index = index * size + c
    return index


def _shift_route(dim, step):
    route = []
    for b in range(_blk_index(tuple(s - 1 for s in BLK_DIMS)) + 1):
        coords = list(_blk_coords(b))
        coords[dim] = (coords[dim] + step) % BLK_DIMS[dim]
        route.append((b, _blk_index(tuple(coords))))
    return route


def _take(data, lead, axis, index):
    offset = len(lead)
    starts = [0] * data.ndim
    sizes = list(data.shape)
    for i, v in enumerate(lead):
        starts[i] = v
        sizes[i] = 1
    starts[offset + axis] = index
    sizes[offset + axis] = 1
    piece = lax.dynamic_slice(data, starts, sizes)
    return piece.reshape(
        [s for i, s in enumerate(sizes) if i >= offset and i != offset + axis]
    )


def ring_reduce_scatter(data, axis, dim, direction, coord, lead=()):
    size = BLK_DIMS[dim]
    route = _shift_route(dim, direction)

    def piece(k):
        return _take(data, lead, axis, (coord - direction * (1 + k)) % size)

    send = piece(0)
    for k in range(size - 1):
        arrived = lax.ppermute(send, "blk", route)
        send = arrived + piece(k + 1)
    return send


def direct_reduce_scatter(data, axis, dim, coord):
    size = BLK_DIMS[dim]
    total = lax.dynamic_index_in_dim(data, coord, axis, keepdims=False)
    for shift in range(1, size):
        piece = lax.dynamic_index_in_dim(data, (coord + shift) % size, axis, keepdims=False)
        total = total + lax.ppermute(piece, "blk", _shift_route(dim, shift))
    return total


def pair_reduce_scatter(data, axis, coord):
    route = _shift_route(2, 1)
    other = lax.dynamic_index_in_dim(data, 1 - coord, axis, keepdims=False)
    mine = lax.dynamic_index_in_dim(data, coord, axis, keepdims=False)
    return lax.ppermute(other, "blk", route) + mine


LINE, CORES = 4, 2


def line_all_gather(own):
    z = lax.axis_index("grp") // CORES
    core = lax.axis_index("grp") % CORES
    members = LINE * CORES
    up = [(g, g + CORES) for g in range(members) if g // CORES < LINE - 1]
    down = [(g, g - CORES) for g in range(members) if g // CORES > 0]
    half = own.shape[0] // 2
    chains = []
    for part in (own[:half], own[half:]):
        got_below, got_above = [], []
        send_up, send_down = part, part
        for _ in range(LINE - 1):
            send_up = lax.ppermute(send_up, "grp", up)
            send_down = lax.ppermute(send_down, "grp", down)
            got_below.append(send_up)
            got_above.append(send_down)
        chains.append((jnp.stack(got_below), jnp.stack(got_above)))
    below = jnp.concatenate([chains[0][0], chains[1][0]], axis=1)
    above = jnp.concatenate([chains[0][1], chains[1][1]], axis=1)
    mine = []
    for spot in range(LINE):
        from_below = lax.dynamic_index_in_dim(
            below, jnp.clip(z - 1 - spot, 0, LINE - 2), 0, keepdims=False
        )
        from_above = lax.dynamic_index_in_dim(
            above, jnp.clip(spot - z - 1, 0, LINE - 2), 0, keepdims=False
        )
        mine.append(
            jnp.where(spot == z, own, jnp.where(spot < z, from_below, from_above))
        )
    mine = jnp.stack(mine)
    sibling = [(g, g ^ 1) for g in range(members)]
    theirs = lax.ppermute(mine, "grp", sibling)
    first = jnp.where(core == 0, mine, theirs)
    second = jnp.where(core == 0, theirs, mine)
    gathered = jnp.stack([first, second], axis=1)
    return gathered.reshape((members * own.shape[0],) + own.shape[1:])


def per_device(x_blocks, pair_left, pair_right, pair_target):
    assert lax.axis_size("grp") == LINE * CORES
    gathered = line_all_gather(x_blocks)
    group_count = lax.axis_size("blk")
    assert group_count == BLK_DIMS[0] * BLK_DIMS[1] * BLK_DIMS[2]
    me = lax.axis_index("blk")
    visit = (me - 1 - jnp.arange(group_count, dtype=jnp.int32)) % group_count
    left = jnp.take(pair_left[0, 0], visit, axis=0)
    right = jnp.take(pair_right[0, 0], visit, axis=0)
    target = jnp.take(pair_target[0, 0], visit, axis=0)
    partials = owner_partials(gathered, left, right, target)
    block = x_blocks.shape[1]
    my_y, my_x, my_z = _blk_coords(me)
    firsts = []
    rows = block // ROW_PARTS
    for c in range(CS):
        direction = 1 if c % 2 == 0 else -1
        halves = []
        for h in range(ROW_PARTS):
            part = partials[c * ROW_PARTS + h].reshape(BLK_DIMS + (rows, block))
            if c < 2:
                halves.append(ring_reduce_scatter(part, 1, 1, direction, my_x))
            else:
                halves.append(ring_reduce_scatter(part, 0, 0, direction, my_y))
        firsts.append(jnp.concatenate(halves, axis=-2))
    half = CS // 2
    along_y = direct_reduce_scatter(jnp.stack(firsts[:half]), 1, 0, my_y)
    along_x = direct_reduce_scatter(jnp.stack(firsts[half:]), 1, 1, my_x)
    summed = jnp.concatenate(
        [pair_reduce_scatter(along_y, 1, my_z), pair_reduce_scatter(along_x, 1, my_z)]
    )
    return summed.astype(jnp.bfloat16).reshape(1, 1, CS, block, block)


def solution(mesh):
    return jax.shard_map(
        per_device,
        mesh=mesh,
        in_specs=(
            P(("blk", "grp"), None, None),
            P("blk", "grp", None, None),
            P("blk", "grp", None, None),
            P("blk", "grp", None, None),
        ),
        out_specs=P("blk", "grp", None, None, None),
        check_vma=False,
    )
```

```python
import jax
import jax.numpy as jnp
from jax import lax
from jax.experimental import pallas as pl
from jax.experimental.pallas import tpu as pltpu
from jax.sharding import PartitionSpec as P

CS = 4
OWNERS_PER_STEP = 4
ROW_PARTS = 2


def _products_kernel(left_ref, right_ref, target_ref, x_ref, *refs):
    out_refs, acc_ref = refs[: CS * ROW_PARTS], refs[CS * ROW_PARTS]
    step = pl.program_id(0)
    pair_count = left_ref.shape[0] // (pl.num_programs(0) * OWNERS_PER_STEP)
    acc_ref[...] = jnp.zeros_like(acc_ref)

    def body(j, carry):
        k = j // pair_count
        flat = step * OWNERS_PER_STEP * pair_count + j
        l = left_ref[flat]
        r = right_ref[flat]
        t = target_ref[flat]
        prod = lax.dot_general(
            x_ref[l], x_ref[r], (((0,), (0,)), ((), ())), preferred_element_type=jnp.float32
        )
        acc_ref[t, k] += prod
        return carry

    lax.fori_loop(0, OWNERS_PER_STEP * pair_count, body, 0, unroll=4)
    rows = acc_ref.shape[2] // ROW_PARTS
    for n, out_ref in enumerate(out_refs):
        c, h = divmod(n, ROW_PARTS)
        out_ref[...] = acc_ref[c, :, h * rows : (h + 1) * rows, :]


def owner_partials(gathered, left, right, target):
    owners, pair_count = left.shape
    block = gathered.shape[1]
    steps = owners // OWNERS_PER_STEP
    flops = 2 * owners * pair_count * block * block * block
    return pl.pallas_call(
        _products_kernel,
        out_shape=[jax.ShapeDtypeStruct((owners, block // ROW_PARTS, block), jnp.float32)]
        * (CS * ROW_PARTS),
        grid_spec=pltpu.PrefetchScalarGridSpec(
            num_scalar_prefetch=3,
            grid=(steps,),
            in_specs=[
                pl.BlockSpec(
                    gathered.shape,
                    lambda i, *_: (0, 0, 0),
                    pipeline_mode=pl.Buffered(1),
                )
            ],
            out_specs=[
                pl.BlockSpec(
                    (OWNERS_PER_STEP, block // ROW_PARTS, block), lambda i, *_: (i, 0, 0)
                )
            ]
            * (CS * ROW_PARTS),
            scratch_shapes=[pltpu.VMEM((CS, OWNERS_PER_STEP, block, block), jnp.float32)],
        ),
        compiler_params=pltpu.CompilerParams(
            dimension_semantics=("arbitrary",), vmem_limit_bytes=48 * 1024 * 1024
        ),
        cost_estimate=pl.CostEstimate(
            flops=flops,
            transcendentals=0,
            bytes_accessed=gathered.size * 2 + owners * CS * block * block * 4,
        ),
    )(left.reshape(-1), right.reshape(-1), target.reshape(-1), gathered)


BLK_DIMS = (4, 4, 2)


def _blk_coords(index):
    coords = []
    for size in reversed(BLK_DIMS):
        coords.append(index % size)
        index = index // size
    return tuple(reversed(coords))


def _blk_index(coords):
    index = 0
    for c, size in zip(coords, BLK_DIMS):
        index = index * size + c
    return index


def _shift_route(dim, step):
    route = []
    for b in range(_blk_index(tuple(s - 1 for s in BLK_DIMS)) + 1):
        coords = list(_blk_coords(b))
        coords[dim] = (coords[dim] + step) % BLK_DIMS[dim]
        route.append((b, _blk_index(tuple(coords))))
    return route


def _take(data, lead, axis, index):
    offset = len(lead)
    starts = [0] * data.ndim
    sizes = list(data.shape)
    for i, v in enumerate(lead):
        starts[i] = v
        sizes[i] = 1
    starts[offset + axis] = index
    sizes[offset + axis] = 1
    piece = lax.dynamic_slice(data, starts, sizes)
    return piece.reshape(
        [s for i, s in enumerate(sizes) if i >= offset and i != offset + axis]
    )


def ring_reduce_scatter(data, axis, dim, direction, coord, lead=()):
    size = BLK_DIMS[dim]
    route = _shift_route(dim, direction)

    def piece(k):
        return _take(data, lead, axis, (coord - direction * (1 + k)) % size)

    send = piece(0)
    for k in range(size - 1):
        arrived = lax.ppermute(send, "blk", route)
        send = arrived + piece(k + 1)
    return send


def direct_reduce_scatter(data, axis, dim, coord):
    size = BLK_DIMS[dim]
    total = lax.dynamic_index_in_dim(data, coord, axis, keepdims=False)
    for shift in range(1, size):
        piece = lax.dynamic_index_in_dim(data, (coord + shift) % size, axis, keepdims=False)
        total = total + lax.ppermute(piece, "blk", _shift_route(dim, shift))
    return total


def pair_reduce_scatter(data, axis, coord):
    route = _shift_route(2, 1)
    other = lax.dynamic_index_in_dim(data, 1 - coord, axis, keepdims=False)
    mine = lax.dynamic_index_in_dim(data, coord, axis, keepdims=False)
    return lax.ppermute(other, "blk", route) + mine


LINE, CORES = 4, 2


def line_all_gather(own):
    z = lax.axis_index("grp") // CORES
    core = lax.axis_index("grp") % CORES
    members = LINE * CORES
    up = [(g, g + CORES) for g in range(members) if g // CORES < LINE - 1]
    down = [(g, g - CORES) for g in range(members) if g // CORES > 0]
    half = own.shape[0] // 2
    sibling = [(g, g ^ 1) for g in range(members)]
    pairs = []
    for part in (own[:half], own[half:]):
        got_below, got_above = [], []
        send_up, send_down = part, part
        for _ in range(LINE - 1):
            send_up = lax.ppermute(send_up, "grp", up)
            send_down = lax.ppermute(send_down, "grp", down)
            got_below.append(send_up)
            got_above.append(send_down)
        below = jnp.stack(got_below)
        above = jnp.stack(got_above)
        mine = []
        for spot in range(LINE):
            from_below = lax.dynamic_index_in_dim(
                below, jnp.clip(z - 1 - spot, 0, LINE - 2), 0, keepdims=False
            )
            from_above = lax.dynamic_index_in_dim(
                above, jnp.clip(spot - z - 1, 0, LINE - 2), 0, keepdims=False
            )
            mine.append(
                jnp.where(spot == z, part, jnp.where(spot < z, from_below, from_above))
            )
        mine = jnp.stack(mine)
        theirs = lax.ppermute(mine, "grp", sibling)
        first = jnp.where(core == 0, mine, theirs)
        second = jnp.where(core == 0, theirs, mine)
        pairs.append(jnp.stack([first, second], axis=1))
    gathered = jnp.concatenate(pairs, axis=2)
    return gathered.reshape((members * own.shape[0],) + own.shape[1:])


def per_device(x_blocks, pair_left, pair_right, pair_target):
    assert lax.axis_size("grp") == LINE * CORES
    gathered = line_all_gather(x_blocks)
    group_count = lax.axis_size("blk")
    assert group_count == BLK_DIMS[0] * BLK_DIMS[1] * BLK_DIMS[2]
    me = lax.axis_index("blk")
    visit = (me - 1 - jnp.arange(group_count, dtype=jnp.int32)) % group_count
    left = jnp.take(pair_left[0, 0], visit, axis=0)
    right = jnp.take(pair_right[0, 0], visit, axis=0)
    target = jnp.take(pair_target[0, 0], visit, axis=0)
    partials = owner_partials(gathered, left, right, target)
    block = x_blocks.shape[1]
    my_y, my_x, my_z = _blk_coords(me)
    firsts = []
    rows = block // ROW_PARTS
    for c in range(CS):
        direction = 1 if c % 2 == 0 else -1
        halves = []
        for h in range(ROW_PARTS):
            part = partials[c * ROW_PARTS + h].reshape(BLK_DIMS + (rows, block))
            if c < 2:
                halves.append(ring_reduce_scatter(part, 1, 1, direction, my_x))
            else:
                halves.append(ring_reduce_scatter(part, 0, 0, direction, my_y))
        firsts.append(jnp.concatenate(halves, axis=-2))
    half = CS // 2
    along_y = direct_reduce_scatter(jnp.stack(firsts[:half]), 1, 0, my_y)
    along_x = direct_reduce_scatter(jnp.stack(firsts[half:]), 1, 1, my_x)
    summed = jnp.concatenate(
        [pair_reduce_scatter(along_y, 1, my_z), pair_reduce_scatter(along_x, 1, my_z)]
    )
    return summed.astype(jnp.bfloat16).reshape(1, 1, CS, block, block)


def solution(mesh):
    return jax.shard_map(
        per_device,
        mesh=mesh,
        in_specs=(
            P(("blk", "grp"), None, None),
            P("blk", "grp", None, None),
            P("blk", "grp", None, None),
            P("blk", "grp", None, None),
        ),
        out_specs=P("blk", "grp", None, None, None),
        check_vma=False,
    )
```

```python
import jax
import jax.numpy as jnp
from jax import lax
from jax.experimental import pallas as pl
from jax.experimental.pallas import tpu as pltpu
from jax.sharding import PartitionSpec as P

CS = 4
OWNERS_PER_STEP = 8
ROW_PARTS = 2


def _products_kernel(left_ref, right_ref, target_ref, x_ref, *refs):
    out_refs, acc_ref = refs[: CS * ROW_PARTS], refs[CS * ROW_PARTS]
    step = pl.program_id(0)
    pair_count = left_ref.shape[0] // (pl.num_programs(0) * OWNERS_PER_STEP)
    acc_ref[...] = jnp.zeros_like(acc_ref)

    def body(j, carry):
        k = j // pair_count
        flat = step * OWNERS_PER_STEP * pair_count + j
        l = left_ref[flat]
        r = right_ref[flat]
        t = target_ref[flat]
        prod = lax.dot_general(
            x_ref[l], x_ref[r], (((0,), (0,)), ((), ())), preferred_element_type=jnp.float32
        )
        acc_ref[t, k] += prod
        return carry

    lax.fori_loop(0, OWNERS_PER_STEP * pair_count, body, 0, unroll=4)
    rows = acc_ref.shape[2] // ROW_PARTS
    for n, out_ref in enumerate(out_refs):
        c, h = divmod(n, ROW_PARTS)
        out_ref[...] = acc_ref[c, :, h * rows : (h + 1) * rows, :]


def owner_partials(gathered, left, right, target):
    owners, pair_count = left.shape
    block = gathered.shape[1]
    steps = owners // OWNERS_PER_STEP
    flops = 2 * owners * pair_count * block * block * block
    return pl.pallas_call(
        _products_kernel,
        out_shape=[jax.ShapeDtypeStruct((owners, block // ROW_PARTS, block), jnp.float32)]
        * (CS * ROW_PARTS),
        grid_spec=pltpu.PrefetchScalarGridSpec(
            num_scalar_prefetch=3,
            grid=(steps,),
            in_specs=[
                pl.BlockSpec(
                    gathered.shape,
                    lambda i, *_: (0, 0, 0),
                    pipeline_mode=pl.Buffered(1),
                )
            ],
            out_specs=[
                pl.BlockSpec(
                    (OWNERS_PER_STEP, block // ROW_PARTS, block), lambda i, *_: (i, 0, 0)
                )
            ]
            * (CS * ROW_PARTS),
            scratch_shapes=[pltpu.VMEM((CS, OWNERS_PER_STEP, block, block), jnp.float32)],
        ),
        compiler_params=pltpu.CompilerParams(
            dimension_semantics=("arbitrary",), vmem_limit_bytes=48 * 1024 * 1024
        ),
        cost_estimate=pl.CostEstimate(
            flops=flops,
            transcendentals=0,
            bytes_accessed=gathered.size * 2 + owners * CS * block * block * 4,
        ),
    )(left.reshape(-1), right.reshape(-1), target.reshape(-1), gathered)


BLK_DIMS = (4, 4, 2)


def _blk_coords(index):
    coords = []
    for size in reversed(BLK_DIMS):
        coords.append(index % size)
        index = index // size
    return tuple(reversed(coords))


def _blk_index(coords):
    index = 0
    for c, size in zip(coords, BLK_DIMS):
        index = index * size + c
    return index


def _shift_route(dim, step):
    route = []
    for b in range(_blk_index(tuple(s - 1 for s in BLK_DIMS)) + 1):
        coords = list(_blk_coords(b))
        coords[dim] = (coords[dim] + step) % BLK_DIMS[dim]
        route.append((b, _blk_index(tuple(coords))))
    return route


def _take(data, lead, axis, index):
    offset = len(lead)
    starts = [0] * data.ndim
    sizes = list(data.shape)
    for i, v in enumerate(lead):
        starts[i] = v
        sizes[i] = 1
    starts[offset + axis] = index
    sizes[offset + axis] = 1
    piece = lax.dynamic_slice(data, starts, sizes)
    return piece.reshape(
        [s for i, s in enumerate(sizes) if i >= offset and i != offset + axis]
    )


def ring_reduce_scatter(data, axis, dim, direction, coord, lead=()):
    size = BLK_DIMS[dim]
    route = _shift_route(dim, direction)

    def piece(k):
        return _take(data, lead, axis, (coord - direction * (1 + k)) % size)

    send = piece(0)
    for k in range(size - 1):
        arrived = lax.ppermute(send, "blk", route)
        send = arrived + piece(k + 1)
    return send


def direct_reduce_scatter(data, axis, dim, coord):
    size = BLK_DIMS[dim]
    total = lax.dynamic_index_in_dim(data, coord, axis, keepdims=False)
    for shift in range(1, size):
        piece = lax.dynamic_index_in_dim(data, (coord + shift) % size, axis, keepdims=False)
        total = total + lax.ppermute(piece, "blk", _shift_route(dim, shift))
    return total


def pair_reduce_scatter(data, axis, coord):
    route = _shift_route(2, 1)
    other = lax.dynamic_index_in_dim(data, 1 - coord, axis, keepdims=False)
    mine = lax.dynamic_index_in_dim(data, coord, axis, keepdims=False)
    return lax.ppermute(other, "blk", route) + mine


LINE, CORES = 4, 2


def line_all_gather(own):
    z = lax.axis_index("grp") // CORES
    core = lax.axis_index("grp") % CORES
    members = LINE * CORES
    up = [(g, g + CORES) for g in range(members) if g // CORES < LINE - 1]
    down = [(g, g - CORES) for g in range(members) if g // CORES > 0]
    half = own.shape[0] // 2
    chains = []
    for part in (own[:half], own[half:]):
        got_below, got_above = [], []
        send_up, send_down = part, part
        for _ in range(LINE - 1):
            send_up = lax.ppermute(send_up, "grp", up)
            send_down = lax.ppermute(send_down, "grp", down)
            got_below.append(send_up)
            got_above.append(send_down)
        chains.append((jnp.stack(got_below), jnp.stack(got_above)))
    below = jnp.concatenate([chains[0][0], chains[1][0]], axis=1)
    above = jnp.concatenate([chains[0][1], chains[1][1]], axis=1)
    mine = []
    for spot in range(LINE):
        from_below = lax.dynamic_index_in_dim(
            below, jnp.clip(z - 1 - spot, 0, LINE - 2), 0, keepdims=False
        )
        from_above = lax.dynamic_index_in_dim(
            above, jnp.clip(spot - z - 1, 0, LINE - 2), 0, keepdims=False
        )
        mine.append(
            jnp.where(spot == z, own, jnp.where(spot < z, from_below, from_above))
        )
    mine = jnp.stack(mine)
    sibling = [(g, g ^ 1) for g in range(members)]
    theirs = lax.ppermute(mine, "grp", sibling)
    first = jnp.where(core == 0, mine, theirs)
    second = jnp.where(core == 0, theirs, mine)
    gathered = jnp.stack([first, second], axis=1)
    return gathered.reshape((members * own.shape[0],) + own.shape[1:])


def per_device(x_blocks, pair_left, pair_right, pair_target):
    assert lax.axis_size("grp") == LINE * CORES
    gathered = line_all_gather(x_blocks)
    group_count = lax.axis_size("blk")
    assert group_count == BLK_DIMS[0] * BLK_DIMS[1] * BLK_DIMS[2]
    me = lax.axis_index("blk")
    visit = (me - 1 - jnp.arange(group_count, dtype=jnp.int32)) % group_count
    left = jnp.take(pair_left[0, 0], visit, axis=0)
    right = jnp.take(pair_right[0, 0], visit, axis=0)
    target = jnp.take(pair_target[0, 0], visit, axis=0)
    partials = owner_partials(gathered, left, right, target)
    block = x_blocks.shape[1]
    my_y, my_x, my_z = _blk_coords(me)
    firsts = []
    rows = block // ROW_PARTS
    for c in range(CS):
        direction = 1 if c % 2 == 0 else -1
        halves = []
        for h in range(ROW_PARTS):
            part = partials[c * ROW_PARTS + h].reshape(BLK_DIMS + (rows, block))
            if c < 2:
                halves.append(ring_reduce_scatter(part, 1, 1, direction, my_x))
            else:
                halves.append(ring_reduce_scatter(part, 0, 0, direction, my_y))
        firsts.append(jnp.concatenate(halves, axis=-2))
    half = CS // 2
    along_y = direct_reduce_scatter(jnp.stack(firsts[:half]), 1, 0, my_y)
    along_x = direct_reduce_scatter(jnp.stack(firsts[half:]), 1, 1, my_x)
    summed = jnp.concatenate(
        [pair_reduce_scatter(along_y, 1, my_z), pair_reduce_scatter(along_x, 1, my_z)]
    )
    return summed.astype(jnp.bfloat16).reshape(1, 1, CS, block, block)


def solution(mesh):
    return jax.shard_map(
        per_device,
        mesh=mesh,
        in_specs=(
            P(("blk", "grp"), None, None),
            P("blk", "grp", None, None),
            P("blk", "grp", None, None),
            P("blk", "grp", None, None),
        ),
        out_specs=P("blk", "grp", None, None, None),
        check_vma=False,
    )
```

```python
import jax
import jax.numpy as jnp
from jax import lax
from jax.experimental import pallas as pl
from jax.experimental.pallas import tpu as pltpu
from jax.sharding import PartitionSpec as P

CS = 4
OWNERS_PER_STEP = 4
ROW_PARTS = 2


def _products_kernel(left_ref, right_ref, target_ref, x_ref, *refs):
    out_refs, acc_ref = refs[: CS * ROW_PARTS], refs[CS * ROW_PARTS]
    step = pl.program_id(0)
    pair_count = left_ref.shape[0] // (pl.num_programs(0) * OWNERS_PER_STEP)
    acc_ref[...] = jnp.zeros_like(acc_ref)

    def body(j, carry):
        k = j // pair_count
        flat = step * OWNERS_PER_STEP * pair_count + j
        l = left_ref[flat]
        r = right_ref[flat]
        t = target_ref[flat]
        prod = lax.dot_general(
            x_ref[l], x_ref[r], (((0,), (0,)), ((), ())), preferred_element_type=jnp.float32
        )
        acc_ref[t, k] += prod
        return carry

    lax.fori_loop(0, OWNERS_PER_STEP * pair_count, body, 0, unroll=12)
    rows = acc_ref.shape[2] // ROW_PARTS
    for n, out_ref in enumerate(out_refs):
        c, h = divmod(n, ROW_PARTS)
        out_ref[...] = acc_ref[c, :, h * rows : (h + 1) * rows, :]


def owner_partials(gathered, left, right, target):
    owners, pair_count = left.shape
    block = gathered.shape[1]
    steps = owners // OWNERS_PER_STEP
    flops = 2 * owners * pair_count * block * block * block
    return pl.pallas_call(
        _products_kernel,
        out_shape=[jax.ShapeDtypeStruct((owners, block // ROW_PARTS, block), jnp.float32)]
        * (CS * ROW_PARTS),
        grid_spec=pltpu.PrefetchScalarGridSpec(
            num_scalar_prefetch=3,
            grid=(steps,),
            in_specs=[
                pl.BlockSpec(
                    gathered.shape,
                    lambda i, *_: (0, 0, 0),
                    pipeline_mode=pl.Buffered(1),
                )
            ],
            out_specs=[
                pl.BlockSpec(
                    (OWNERS_PER_STEP, block // ROW_PARTS, block), lambda i, *_: (i, 0, 0)
                )
            ]
            * (CS * ROW_PARTS),
            scratch_shapes=[pltpu.VMEM((CS, OWNERS_PER_STEP, block, block), jnp.float32)],
        ),
        compiler_params=pltpu.CompilerParams(
            dimension_semantics=("arbitrary",), vmem_limit_bytes=48 * 1024 * 1024
        ),
        cost_estimate=pl.CostEstimate(
            flops=flops,
            transcendentals=0,
            bytes_accessed=gathered.size * 2 + owners * CS * block * block * 4,
        ),
    )(left.reshape(-1), right.reshape(-1), target.reshape(-1), gathered)


BLK_DIMS = (4, 4, 2)


def _blk_coords(index):
    coords = []
    for size in reversed(BLK_DIMS):
        coords.append(index % size)
        index = index // size
    return tuple(reversed(coords))


def _blk_index(coords):
    index = 0
    for c, size in zip(coords, BLK_DIMS):
        index = index * size + c
    return index


def _shift_route(dim, step):
    route = []
    for b in range(_blk_index(tuple(s - 1 for s in BLK_DIMS)) + 1):
        coords = list(_blk_coords(b))
        coords[dim] = (coords[dim] + step) % BLK_DIMS[dim]
        route.append((b, _blk_index(tuple(coords))))
    return route


def _take(data, lead, axis, index):
    offset = len(lead)
    starts = [0] * data.ndim
    sizes = list(data.shape)
    for i, v in enumerate(lead):
        starts[i] = v
        sizes[i] = 1
    starts[offset + axis] = index
    sizes[offset + axis] = 1
    piece = lax.dynamic_slice(data, starts, sizes)
    return piece.reshape(
        [s for i, s in enumerate(sizes) if i >= offset and i != offset + axis]
    )


def ring_reduce_scatter(data, axis, dim, direction, coord, lead=()):
    size = BLK_DIMS[dim]
    route = _shift_route(dim, direction)

    def piece(k):
        return _take(data, lead, axis, (coord - direction * (1 + k)) % size)

    send = piece(0)
    for k in range(size - 1):
        arrived = lax.ppermute(send, "blk", route)
        send = arrived + piece(k + 1)
    return send


def direct_reduce_scatter(data, axis, dim, coord):
    size = BLK_DIMS[dim]
    total = lax.dynamic_index_in_dim(data, coord, axis, keepdims=False)
    for shift in range(1, size):
        piece = lax.dynamic_index_in_dim(data, (coord + shift) % size, axis, keepdims=False)
        total = total + lax.ppermute(piece, "blk", _shift_route(dim, shift))
    return total


def pair_reduce_scatter(data, axis, coord):
    route = _shift_route(2, 1)
    other = lax.dynamic_index_in_dim(data, 1 - coord, axis, keepdims=False)
    mine = lax.dynamic_index_in_dim(data, coord, axis, keepdims=False)
    return lax.ppermute(other, "blk", route) + mine


LINE, CORES = 4, 2


def line_all_gather(own):
    z = lax.axis_index("grp") // CORES
    core = lax.axis_index("grp") % CORES
    members = LINE * CORES
    up = [(g, g + CORES) for g in range(members) if g // CORES < LINE - 1]
    down = [(g, g - CORES) for g in range(members) if g // CORES > 0]
    half = own.shape[0] // 2
    chains = []
    for part in (own[:half], own[half:]):
        got_below, got_above = [], []
        send_up, send_down = part, part
        for _ in range(LINE - 1):
            send_up = lax.ppermute(send_up, "grp", up)
            send_down = lax.ppermute(send_down, "grp", down)
            got_below.append(send_up)
            got_above.append(send_down)
        chains.append((jnp.stack(got_below), jnp.stack(got_above)))
    below = jnp.concatenate([chains[0][0], chains[1][0]], axis=1)
    above = jnp.concatenate([chains[0][1], chains[1][1]], axis=1)
    mine = []
    for spot in range(LINE):
        from_below = lax.dynamic_index_in_dim(
            below, jnp.clip(z - 1 - spot, 0, LINE - 2), 0, keepdims=False
        )
        from_above = lax.dynamic_index_in_dim(
            above, jnp.clip(spot - z - 1, 0, LINE - 2), 0, keepdims=False
        )
        mine.append(
            jnp.where(spot == z, own, jnp.where(spot < z, from_below, from_above))
        )
    mine = jnp.stack(mine)
    sibling = [(g, g ^ 1) for g in range(members)]
    theirs = lax.ppermute(mine, "grp", sibling)
    first = jnp.where(core == 0, mine, theirs)
    second = jnp.where(core == 0, theirs, mine)
    gathered = jnp.stack([first, second], axis=1)
    return gathered.reshape((members * own.shape[0],) + own.shape[1:])


def per_device(x_blocks, pair_left, pair_right, pair_target):
    assert lax.axis_size("grp") == LINE * CORES
    gathered = line_all_gather(x_blocks)
    group_count = lax.axis_size("blk")
    assert group_count == BLK_DIMS[0] * BLK_DIMS[1] * BLK_DIMS[2]
    me = lax.axis_index("blk")
    visit = (me - 1 - jnp.arange(group_count, dtype=jnp.int32)) % group_count
    left = jnp.take(pair_left[0, 0], visit, axis=0)
    right = jnp.take(pair_right[0, 0], visit, axis=0)
    target = jnp.take(pair_target[0, 0], visit, axis=0)
    partials = owner_partials(gathered, left, right, target)
    block = x_blocks.shape[1]
    my_y, my_x, my_z = _blk_coords(me)
    firsts = []
    rows = block // ROW_PARTS
    for c in range(CS):
        direction = 1 if c % 2 == 0 else -1
        halves = []
        for h in range(ROW_PARTS):
            part = partials[c * ROW_PARTS + h].reshape(BLK_DIMS + (rows, block))
            if c < 2:
                halves.append(ring_reduce_scatter(part, 1, 1, direction, my_x))
            else:
                halves.append(ring_reduce_scatter(part, 0, 0, direction, my_y))
        firsts.append(jnp.concatenate(halves, axis=-2))
    half = CS // 2
    along_y = direct_reduce_scatter(jnp.stack(firsts[:half]), 1, 0, my_y)
    along_x = direct_reduce_scatter(jnp.stack(firsts[half:]), 1, 1, my_x)
    summed = jnp.concatenate(
        [pair_reduce_scatter(along_y, 1, my_z), pair_reduce_scatter(along_x, 1, my_z)]
    )
    return summed.astype(jnp.bfloat16).reshape(1, 1, CS, block, block)


def solution(mesh):
    return jax.shard_map(
        per_device,
        mesh=mesh,
        in_specs=(
            P(("blk", "grp"), None, None),
            P("blk", "grp", None, None),
            P("blk", "grp", None, None),
            P("blk", "grp", None, None),
        ),
        out_specs=P("blk", "grp", None, None, None),
        check_vma=False,
    )
```
